1024 devices in a mesh: morton: 16 (over z, core), slab: 64 (over x, y).
Axes of the slice: x: 8, y: 8, z: 8, core: 2. Of those that a mesh axis runs over, the one named last changes fastest.
Arguments:
- velocity: float32 [1024, 256, 256], P('slab', 'morton'), may hold values from -6 to 6
Outputs:
- approx: float32 [256, 64, 64], P('slab', 'morton')
- detail_two: float32 [7, 256, 64, 64], P(None, 'slab', 'morton')
- detail_one: float32 [7, 512, 128, 128], P(None, 'slab', 'morton')
The draws below stay inside these ranges and needn't reach their ends.
All inputs are finite; a program needn't handle non-finite values.
Results may differ from the reference program's by a relative error of at most 0.00002.
Values sent between devices are 32-bit elements; how exact they have to be, the bound alone decides.
No kernel may reach another device: no remote copies, remote signals or barrier semaphores. Data moves between devices by JAX's collectives and lax.ppermute only.
A program may use at most 32 MiB of HBM per device.

```python
import jax
import jax.numpy as jnp
from jax import lax

NZ = 256
NX = 1024
NY = 256


def block_levels(stream_key, dims, shards, low, top_value):
    gain, own = 1.0, jax.random.fold_in(stream_key, 6)
    for axis_at, parts in shards:
        heights = jnp.exp(jax.random.uniform(jax.random.fold_in(own, axis_at), (parts,), jnp.float32, low / len(shards), top_value / len(shards)))
        gain = gain * jnp.repeat(heights, dims[axis_at] // parts).reshape([-1 if axis == axis_at else 1 for axis in range(len(dims))])
    return gain


def bell_draw(key, extent, spread, limit, pieces=(), kind=jnp.bfloat16):
    gain = block_levels(key, extent, pieces, -0.22, 0.18) if pieces else 1.0
    drawn = jax.random.normal(key, extent, jnp.float32) * spread * gain
    return jnp.minimum(jnp.maximum(drawn, -limit), limit).astype(kind)


def setup_inputs(seed: int = 0) -> dict:
    key_of = jax.random.split(jax.random.key(seed), 2)
    return {
        "velocity": bell_draw(key_of[0], (NX, NY, NZ), 1.0, 6.0, ((0, 64), (1, 16)), jnp.float32),
    }


LIFT_ALPHA = -1.586134342059924
LIFT_BETA = -0.052980118572961
LIFT_GAMMA = 0.882911075530934
LIFT_DELTA = 0.443506852043971
LIFT_SCALE = 1.149604398860241


def cut_range(values, start, stop, dimension):
    return lax.slice_in_dim(values, start, stop, axis=dimension)


def lifting(extended, dimension):
    halfway = extended.shape[dimension] // 2
    new_shape = extended.shape[:dimension] + (halfway, 2) + extended.shape[dimension + 1:]
    paired = extended.reshape(new_shape)
    even_part = lax.index_in_dim(paired, 0, dimension + 1, keepdims=False)
    odd_part = lax.index_in_dim(paired, 1, dimension + 1, keepdims=False)
    first_detail = cut_range(odd_part, 0, halfway - 1, dimension) + LIFT_ALPHA * (
        cut_range(even_part, 0, halfway - 1, dimension) + cut_range(even_part, 1, halfway, dimension))
    first_smooth = cut_range(even_part, 1, halfway - 1, dimension) + LIFT_BETA * (
        cut_range(first_detail, 0, halfway - 2, dimension) + cut_range(first_detail, 1, halfway - 1, dimension))
    second_detail = cut_range(first_detail, 1, halfway - 2, dimension) + LIFT_GAMMA * (
        cut_range(first_smooth, 0, halfway - 3, dimension) + cut_range(first_smooth, 1, halfway - 2, dimension))
    second_smooth = cut_range(first_smooth, 1, halfway - 3, dimension) + LIFT_DELTA * (
        cut_range(second_detail, 0, halfway - 4, dimension) + cut_range(second_detail, 1, halfway - 3, dimension))
    lowpass = second_smooth * LIFT_SCALE
    highpass = cut_range(second_detail, 1, halfway - 3, dimension) / LIFT_SCALE
    return lowpass, highpass


def mirrored(values, dimension):
    widths = [(0, 0)] * values.ndim
    widths[dimension] = (4, 4)
    return jnp.pad(values, widths, mode="reflect")


def one_level(volume):
    subbands = [volume]
    for dimension in range(3):
        refined = []
        for subband in subbands:
            lowpass, highpass = lifting(mirrored(subband, dimension), dimension)
            refined = refined + [lowpass, highpass]
        subbands = refined
    return subbands


def reference(velocity):
    level_one = one_level(velocity)
    level_two = one_level(level_one[0])
    return level_two[0], jnp.stack(level_two[1:]), jnp.stack(level_one[1:])
```

```python
import jax
import jax.numpy as jnp
from jax import lax
from jax.sharding import PartitionSpec as P

LIFT_ALPHA = -1.586134342059924
LIFT_BETA = -0.052980118572961
LIFT_GAMMA = 0.882911075530934
LIFT_DELTA = 0.443506852043971
LIFT_SCALE = 1.149604398860241

WIDE = 12
NARROW = 4


def cut_range(values, start, stop, dimension):
    return lax.slice_in_dim(values, start, stop, axis=dimension)


def lifting(extended, dimension):
    halfway = extended.shape[dimension] // 2
    new_shape = extended.shape[:dimension] + (halfway, 2) + extended.shape[dimension + 1 :]
    paired = extended.reshape(new_shape)
    even_part = lax.index_in_dim(paired, 0, dimension + 1, keepdims=False)
    odd_part = lax.index_in_dim(paired, 1, dimension + 1, keepdims=False)
    first_detail = cut_range(odd_part, 0, halfway - 1, dimension) + LIFT_ALPHA * (
        cut_range(even_part, 0, halfway - 1, dimension)
        + cut_range(even_part, 1, halfway, dimension)
    )
    first_smooth = cut_range(even_part, 1, halfway - 1, dimension) + LIFT_BETA * (
        cut_range(first_detail, 0, halfway - 2, dimension)
        + cut_range(first_detail, 1, halfway - 1, dimension)
    )
    second_detail = cut_range(first_detail, 1, halfway - 2, dimension) + LIFT_GAMMA * (
        cut_range(first_smooth, 0, halfway - 3, dimension)
        + cut_range(first_smooth, 1, halfway - 2, dimension)
    )
    second_smooth = cut_range(first_smooth, 1, halfway - 3, dimension) + LIFT_DELTA * (
        cut_range(second_detail, 0, halfway - 4, dimension)
        + cut_range(second_detail, 1, halfway - 3, dimension)
    )
    lowpass = second_smooth * LIFT_SCALE
    highpass = cut_range(second_detail, 1, halfway - 3, dimension) / LIFT_SCALE
    return (lowpass, highpass)


def part_of(block, offset, width, dimension):
    length = block.shape[dimension]
    if offset < 0:
        return cut_range(block, length - width, length, dimension)
    if offset > 0:
        return cut_range(block, 0, width, dimension)
    return block


def halo_pieces(wide, narrow):
    slabs, bricks = lax.axis_size("slab"), lax.axis_size("morton")
    received = {}
    for ox in (-1, 0, 1):
        for oy in (-1, 0, 1):
            if ox == 0 and oy == 0:
                continue
            pieces = []
            shapes = []
            for block, width in ((wide, WIDE), (narrow, NARROW)):
                piece = part_of(part_of(block, ox, width, 0), oy, width, 1)
                shapes.append(piece.shape)
                pieces.append(piece.reshape(-1, piece.shape[-1]))
            message = jnp.concatenate(pieces, axis=0)
            pairs = []
            for s in range(slabs):
                for m in range(bricks):
                    s_from, m_from = s + ox, m + oy
                    if 0 <= s_from < slabs and 0 <= m_from < bricks:
                        pairs.append((m_from * slabs + s_from, m * slabs + s))
            arrived = lax.ppermute(message, ("morton", "slab"), pairs)
            rows = [shapes[0][0] * shapes[0][1], shapes[1][0] * shapes[1][1]]
            received[(ox, oy)] = (
                arrived[: rows[0]].reshape(shapes[0]),
                arrived[rows[0] :].reshape(shapes[1]),
            )
    return received


def assemble(block, received, which):
    rows = []
    for ox in (-1, 0, 1):
        row = []
        for oy in (-1, 0, 1):
            row.append(block if ox == 0 and oy == 0 else received[(ox, oy)][which])
        rows.append(jnp.concatenate(row, axis=1))
    return jnp.concatenate(rows, axis=0)


def mirror_edges(extended, dimension, width, at_low, at_high, whole):
    length = extended.shape[dimension]
    shift = 1 if whole else 0
    low_mirror = jnp.flip(cut_range(extended, width + shift, 2 * width + shift, dimension), dimension)
    high_mirror = jnp.flip(
        cut_range(extended, length - 2 * width - shift, length - width - shift, dimension), dimension
    )
    leading = jnp.where(at_low, low_mirror, cut_range(extended, 0, width, dimension))
    trailing = jnp.where(at_high, high_mirror, cut_range(extended, length - width, length, dimension))
    middle = cut_range(extended, width, length - width, dimension)
    return jnp.concatenate([leading, middle, trailing], axis=dimension)


def per_device(velocity):
    slab_low = lax.axis_index("slab") == 0
    slab_high = lax.axis_index("slab") == lax.axis_size("slab") - 1
    brick_low = lax.axis_index("morton") == 0
    brick_high = lax.axis_index("morton") == lax.axis_size("morton") - 1

    padded = jnp.pad(velocity, ((0, 0), (0, 0), (4, 4)), mode="reflect")
    z_low, z_high = lifting(padded, 2)
    received = halo_pieces(z_low, z_high)

    wide = assemble(z_low, received, 0)
    wide = mirror_edges(wide, 1, WIDE, brick_low, brick_high, True)
    wide = mirror_edges(wide, 0, WIDE, slab_low, slab_high, True)
    narrow = assemble(z_high, received, 1)
    narrow = mirror_edges(narrow, 1, NARROW, brick_low, brick_high, True)
    narrow = mirror_edges(narrow, 0, NARROW, slab_low, slab_high, True)

    x_low, x_high = lifting(wide, 0)
    n_rows = velocity.shape[0] // 2
    n_cols = velocity.shape[1] // 2
    inner = slice(4, 4 + n_rows)
    window = slice(WIDE - 4, WIDE + 2 * n_cols + 4)
    coarse, band_2 = lifting(x_low, 1)
    band_2 = band_2[inner, 4 : 4 + n_cols]
    band_4, band_6 = lifting(x_high[inner, window], 1)
    xn_low, xn_high = lifting(narrow, 0)
    band_1, band_3 = lifting(xn_low, 1)
    band_5, band_7 = lifting(xn_high, 1)
    detail_one = jnp.stack([band_1, band_2, band_3, band_4, band_5, band_6, band_7])

    coarse = mirror_edges(coarse, 0, 4, slab_low, slab_high, True)
    coarse = mirror_edges(coarse, 1, 4, brick_low, brick_high, True)
    level_two = []
    for x_band in lifting(coarse, 0):
        for y_band in lifting(x_band, 1):
            padded = jnp.pad(y_band, ((0, 0), (0, 0), (4, 4)), mode="reflect")
            level_two.extend(lifting(padded, 2))
    return (level_two[0], jnp.stack(level_two[1:]), detail_one)


def solution(mesh):
    placed = (P("slab", "morton", None),)
    return jax.shard_map(
        per_device,
        mesh=mesh,
        in_specs=placed,
        out_specs=(
            P("slab", "morton", None),
            P(None, "slab", "morton", None),
            P(None, "slab", "morton", None),
        ),
        check_vma=False,
    )
```

```python
import numpy as np
import jax
import jax.numpy as jnp
from jax import lax
from jax.sharding import PartitionSpec as P

LIFT_ALPHA = -1.586134342059924
LIFT_BETA = -0.052980118572961
LIFT_GAMMA = 0.882911075530934
LIFT_DELTA = 0.443506852043971
LIFT_SCALE = 1.149604398860241

EXACT = lax.Precision.HIGHEST


def lift_rows(signal):
    extended = np.pad(signal, ((4, 4), (0, 0)), mode="reflect")
    even, odd = extended[0::2], extended[1::2]
    first_detail = odd[:-1] + LIFT_ALPHA * (even[:-1] + even[1:])
    first_smooth = even[1:-1] + LIFT_BETA * (first_detail[:-1] + first_detail[1:])
    second_detail = first_detail[1:-1] + LIFT_GAMMA * (first_smooth[:-1] + first_smooth[1:])
    second_smooth = first_smooth[1:-1] + LIFT_DELTA * (second_detail[:-1] + second_detail[1:])
    return second_smooth * LIFT_SCALE, second_detail[1:] / LIFT_SCALE


def level_maps(length):
    low, high = lift_rows(np.eye(length))
    low_two, high_two = lift_rows(low)
    return (low, high), (low_two, high_two)


def window_maps(block, halo, level, blocks=8):
    length = block * blocks
    bands = level_maps(length)[level]
    share = block // (2 * (level + 1))
    width = halo[0] + block + halo[1]
    maps = []
    for place in (0, blocks // 2, blocks - 1):
        rows = np.concatenate([band[place * share : (place + 1) * share] for band in bands])
        matrix = np.zeros((rows.shape[0], width))
        for i in range(width):
            cell = place * block - halo[0] + i
            if 0 <= cell < length:
                matrix[:, i] = rows[:, cell]
        maps.append(matrix.astype(np.float32))
    return maps


def chosen(maps, at_low, at_high):
    low, inside, high = (jnp.asarray(m) for m in maps)
    return jnp.where(at_low, low, jnp.where(at_high, high, inside))


def exchange(lower_half, upper_half, axis):
    devices = lax.axis_size(axis)
    up = [(i, i + 1) for i in range(devices - 1)]
    down = [(i + 1, i) for i in range(devices - 1)]
    from_below = lax.ppermute(upper_half, axis, up)
    from_above = lax.ppermute(lower_half, axis, down)
    return from_below, from_above


def per_device(velocity):
    nx, ny, nz = velocity.shape
    slab_low = lax.axis_index("slab") == 0
    slab_high = lax.axis_index("slab") == lax.axis_size("slab") - 1
    brick_low = lax.axis_index("morton") == 0
    brick_high = lax.axis_index("morton") == lax.axis_size("morton") - 1

    (z_low, z_high), (z2_low, z2_high) = level_maps(nz)
    z_maps = np.stack([z_low.T, z_high.T, np.concatenate([z2_low, z2_high]).T]).astype(np.float32)
    lanes = z_maps.shape[2]
    u = jnp.einsum("xyz,bzk->xbyk", velocity, jnp.asarray(z_maps), precision=EXACT)

    wide = 12
    one_rows = u[:, 0:2]
    two_rows = u[:, 2]
    flat = lambda a: a.reshape(-1, lanes)
    top = jnp.concatenate([flat(one_rows[nx - 4 :]), flat(two_rows[nx - wide :])])
    bottom = jnp.concatenate([flat(one_rows[:4]), flat(two_rows[:wide])])
    below, above = exchange(bottom, top, "slab")
    split = 4 * 2 * ny
    one_ext = jnp.concatenate(
        [below[:split].reshape(4, 2, ny, lanes), one_rows, above[:split].reshape(4, 2, ny, lanes)]
    )
    two_ext = jnp.concatenate(
        [below[split:].reshape(wide, ny, lanes), two_rows, above[split:].reshape(wide, ny, lanes)]
    )
    a1x = chosen(window_maps(nx, (4, 4), 0), slab_low, slab_high)
    a2x = chosen(window_maps(nx, (wide, wide), 1), slab_low, slab_high)
    x_one = jnp.einsum("kx,xbyz->kbyz", a1x, one_ext, precision=EXACT)
    x_two = jnp.einsum("kx,xyz->kyz", a2x, two_ext, precision=EXACT)

    narrow = 8
    kx1, kx2 = x_one.shape[0], x_two.shape[0]
    top = jnp.concatenate([flat(x_one[:, :, ny - narrow :]), flat(x_two)])
    bottom = jnp.concatenate([flat(x_one[:, :, :narrow]), flat(x_two)])
    below, above = exchange(bottom, top, "morton")
    split = kx1 * 2 * narrow
    one_ext = jnp.concatenate(
        [
            below[:split].reshape(kx1, 2, narrow, lanes),
            x_one,
            above[:split].reshape(kx1, 2, narrow, lanes),
        ],
        axis=2,
    )
    two_ext = jnp.concatenate(
        [below[split:].reshape(kx2, ny, lanes), x_two, above[split:].reshape(kx2, ny, lanes)],
        axis=1,
    )
    a1y = chosen(window_maps(ny, (narrow, narrow), 0), brick_low, brick_high)
    a2y = chosen(window_maps(ny, (ny, ny), 1), brick_low, brick_high)
    y_one = jnp.einsum("ky,abyz->abkz", a1y, one_ext, precision=EXACT)
    y_two = jnp.einsum("ky,ayz->akz", a2y, two_ext, precision=EXACT)

    hx, hy = nx // 2, ny // 2
    level_one = y_one.reshape(2, hx, 2, 2, hy, lanes).transpose(0, 3, 2, 1, 4, 5)
    level_one = level_one.reshape(8, hx, hy, lanes)
    qx, qy, qz = nx // 4, ny // 4, nz // 4
    level_two = y_two.reshape(2, qx, 2, qy, 2, qz).transpose(0, 2, 4, 1, 3, 5)
    level_two = level_two.reshape(8, qx, qy, qz)
    return (level_two[0], level_two[1:], level_one[1:])


def solution(mesh):
    placed = (P("slab", "morton", None),)
    return jax.shard_map(
        per_device,
        mesh=mesh,
        in_specs=placed,
        out_specs=(
            P("slab", "morton", None),
            P(None, "slab", "morton", None),
            P(None, "slab", "morton", None),
        ),
        check_vma=False,
    )
```

```python
import numpy as np
import jax
import jax.numpy as jnp
from jax import lax
from jax.sharding import PartitionSpec as P

LIFT_ALPHA = -1.586134342059924
LIFT_BETA = -0.052980118572961
LIFT_GAMMA = 0.882911075530934
LIFT_DELTA = 0.443506852043971
LIFT_SCALE = 1.149604398860241

EXACT = lax.Precision.HIGHEST


def lift_rows(signal):
    extended = np.pad(signal, ((4, 4), (0, 0)), mode="reflect")
    even, odd = extended[0::2], extended[1::2]
    first_detail = odd[:-1] + LIFT_ALPHA * (even[:-1] + even[1:])
    first_smooth = even[1:-1] + LIFT_BETA * (first_detail[:-1] + first_detail[1:])
    second_detail = first_detail[1:-1] + LIFT_GAMMA * (first_smooth[:-1] + first_smooth[1:])
    second_smooth = first_smooth[1:-1] + LIFT_DELTA * (second_detail[:-1] + second_detail[1:])
    return second_smooth * LIFT_SCALE, second_detail[1:] / LIFT_SCALE


def level_maps(length):
    low, high = lift_rows(np.eye(length))
    low_two, high_two = lift_rows(low)
    return (low, high), (low_two, high_two)


def window_maps(block, halo, level, blocks=8):
    length = block * blocks
    bands = level_maps(length)[level]
    share = block // (2 * (level + 1))
    width = halo[0] + block + halo[1]
    maps = []
    for place in (0, blocks // 2, blocks - 1):
        rows = np.concatenate([band[place * share : (place + 1) * share] for band in bands])
        matrix = np.zeros((rows.shape[0], width))
        for i in range(width):
            cell = place * block - halo[0] + i
            if 0 <= cell < length:
                matrix[:, i] = rows[:, cell]
        maps.append(matrix.astype(np.float32))
    return maps


def chosen(maps, at_low, at_high):
    low, inside, high = (jnp.asarray(m) for m in maps)
    return jnp.where(at_low, low, jnp.where(at_high, high, inside))


def neighbours(pieces_of):
    slabs, bricks = lax.axis_size("slab"), lax.axis_size("morton")
    received = {}
    for ox in (-1, 0, 1):
        for oy in (-1, 0, 1):
            if ox == 0 and oy == 0:
                continue
            pieces = pieces_of(ox, oy)
            message = jnp.concatenate([p.reshape(-1, p.shape[-1]) for p in pieces])
            pairs = []
            for s in range(slabs):
                for m in range(bricks):
                    s_from, m_from = s + ox, m + oy
                    if 0 <= s_from < slabs and 0 <= m_from < bricks:
                        pairs.append((m_from * slabs + s_from, m * slabs + s))
            arrived = lax.ppermute(message, ("morton", "slab"), pairs)
            unpacked, at = [], 0
            for p in pieces:
                rows = p.size // p.shape[-1]
                unpacked.append(arrived[at : at + rows].reshape(p.shape))
                at += rows
            received[(ox, oy)] = unpacked
    return received


def edge(block, offset, width, dimension):
    length = block.shape[dimension]
    if offset < 0:
        return lax.slice_in_dim(block, length - width, length, axis=dimension)
    if offset > 0:
        return lax.slice_in_dim(block, 0, width, axis=dimension)
    return block


def assemble(own, received, which, x_dim, y_dim):
    rows = []
    for ox in (-1, 0, 1):
        row = [own if ox == 0 and oy == 0 else received[(ox, oy)][which] for oy in (-1, 0, 1)]
        rows.append(jnp.concatenate(row, axis=y_dim))
    return jnp.concatenate(rows, axis=x_dim)


def per_device(velocity):
    nx, ny, nz = velocity.shape
    slab_low = lax.axis_index("slab") == 0
    slab_high = lax.axis_index("slab") == lax.axis_size("slab") - 1
    brick_low = lax.axis_index("morton") == 0
    brick_high = lax.axis_index("morton") == lax.axis_size("morton") - 1

    (z_low, z_high), (z2_low, z2_high) = level_maps(nz)
    z_maps = np.stack([z_low.T, z_high.T, np.concatenate([z2_low, z2_high]).T]).astype(np.float32)
    lanes = z_maps.shape[2]
    u = jnp.einsum("xyz,bzk->xbyk", velocity, jnp.asarray(z_maps), precision=EXACT)
    one = u[:, 0:2]
    two = u[:, 2]

    rows_one, rows_two, cols_one, cols_two = 4, 12, 8, ny

    def pieces_of(ox, oy):
        return [
            edge(edge(one, ox, rows_one, 0), oy, cols_one, 2),
            edge(edge(two, ox, rows_two, 0), oy, cols_two, 1),
        ]

    received = neighbours(pieces_of)
    one_ext = assemble(one, received, 0, 0, 2)
    two_ext = assemble(two, received, 1, 0, 1)

    a1x = chosen(window_maps(nx, (rows_one, rows_one), 0), slab_low, slab_high)
    a2x = chosen(window_maps(nx, (rows_two, rows_two), 1), slab_low, slab_high)
    a1y = chosen(window_maps(ny, (cols_one, cols_one), 0), brick_low, brick_high)
    a2y = chosen(window_maps(ny, (cols_two, cols_two), 1), brick_low, brick_high)
    x_one = jnp.einsum("kx,xbyz->kbyz", a1x, one_ext, precision=EXACT)
    x_two = jnp.einsum("kx,xyz->kyz", a2x, two_ext, precision=EXACT)
    y_one = jnp.einsum("ky,abyz->abkz", a1y, x_one, precision=EXACT)
    y_two = jnp.einsum("ky,ayz->akz", a2y, x_two, precision=EXACT)

    hx, hy = nx // 2, ny // 2
    level_one = y_one.reshape(2, hx, 2, 2, hy, lanes).transpose(0, 3, 2, 1, 4, 5)
    level_one = level_one.reshape(8, hx, hy, lanes)
    qx, qy, qz = nx // 4, ny // 4, nz // 4
    level_two = y_two.reshape(2, qx, 2, qy, 2, qz).transpose(0, 2, 4, 1, 3, 5)
    level_two = level_two.reshape(8, qx, qy, qz)
    return (level_two[0], level_two[1:], level_one[1:])


def solution(mesh):
    placed = (P("slab", "morton", None),)
    return jax.shard_map(
        per_device,
        mesh=mesh,
        in_specs=placed,
        out_specs=(
            P("slab", "morton", None),
            P(None, "slab", "morton", None),
            P(None, "slab", "morton", None),
        ),
        check_vma=False,
    )
```

```python
import numpy as np
import jax
import jax.numpy as jnp
from jax import lax
from jax.sharding import PartitionSpec as P

LIFT_ALPHA = -1.586134342059924
LIFT_BETA = -0.052980118572961
LIFT_GAMMA = 0.882911075530934
LIFT_DELTA = 0.443506852043971
LIFT_SCALE = 1.149604398860241

EXACT = lax.Precision.HIGHEST


def lift_rows(signal):
    extended = np.pad(signal, ((4, 4), (0, 0)), mode="reflect")
    even, odd = extended[0::2], extended[1::2]
    first_detail = odd[:-1] + LIFT_ALPHA * (even[:-1] + even[1:])
    first_smooth = even[1:-1] + LIFT_BETA * (first_detail[:-1] + first_detail[1:])
    second_detail = first_detail[1:-1] + LIFT_GAMMA * (first_smooth[:-1] + first_smooth[1:])
    second_smooth = first_smooth[1:-1] + LIFT_DELTA * (second_detail[:-1] + second_detail[1:])
    return second_smooth * LIFT_SCALE, second_detail[1:] / LIFT_SCALE


def level_maps(length):
    low, high = lift_rows(np.eye(length))
    low_two, high_two = lift_rows(low)
    return (low, high), (low_two, high_two)


def window_maps(block, halo, level, blocks=8):
    length = block * blocks
    bands = level_maps(length)[level]
    share = block // (2 * (level + 1))
    width = halo[0] + block + halo[1]
    maps = []
    for place in (0, blocks // 2, blocks - 1):
        rows = np.concatenate([band[place * share : (place + 1) * share] for band in bands])
        matrix = np.zeros((rows.shape[0], width))
        for i in range(width):
            cell = place * block - halo[0] + i
            if 0 <= cell < length:
                matrix[:, i] = rows[:, cell]
        maps.append(matrix.astype(np.float32))
    return maps


def packed_maps(block):
    parts = [
        window_maps(block, (4, 4), 0),
        window_maps(block, (12, 12), 1),
        window_maps(block, (8, 8), 0),
        window_maps(block, (block, block), 1),
    ]
    height = sum(p[0].shape[0] for p in parts)
    width = -(-max(p[0].shape[1] for p in parts) // 128) * 128
    table = np.zeros((3, height, width), np.float32)
    places, row = [], 0
    for p in parts:
        rows, cols = p[0].shape
        for case in range(3):
            table[case, row : row + rows, :cols] = p[case]
        places.append((row, rows, cols))
        row += rows
    return table, places


def case_of(axis):
    index = lax.axis_index(axis)
    last = lax.axis_size(axis) - 1
    return jnp.where(index == 0, 0, jnp.where(index == last, 2, 1))


def exchange(lower_half, upper_half, axis):
    devices = lax.axis_size(axis)
    up = [(i, i + 1) for i in range(devices - 1)]
    down = [(i + 1, i) for i in range(devices - 1)]
    from_below = lax.ppermute(upper_half, axis, up)
    from_above = lax.ppermute(lower_half, axis, down)
    return from_below, from_above


def per_device(velocity):
    nx, ny, nz = velocity.shape

    (z_low, z_high), (z2_low, z2_high) = level_maps(nz)
    z_maps = np.stack([z_low.T, z_high.T, np.concatenate([z2_low, z2_high]).T]).astype(np.float32)
    lanes = z_maps.shape[2]
    u = jnp.einsum("xyz,bzk->xbyk", velocity, jnp.asarray(z_maps), precision=EXACT)

    wide = 12
    one_rows = u[:, 0:2]
    two_rows = u[:, 2]
    flat = lambda a: a.reshape(-1, lanes)
    top = jnp.concatenate([flat(one_rows[nx - 4 :]), flat(two_rows[nx - wide :])])
    bottom = jnp.concatenate([flat(one_rows[:4]), flat(two_rows[:wide])])
    below, above = exchange(bottom, top, "slab")
    split = 4 * 2 * ny
    one_ext = jnp.concatenate(
        [below[:split].reshape(4, 2, ny, lanes), one_rows, above[:split].reshape(4, 2, ny, lanes)]
    )
    two_ext = jnp.concatenate(
        [below[split:].reshape(wide, ny, lanes), two_rows, above[split:].reshape(wide, ny, lanes)]
    )
    assert nx == ny and wide == 12
    table, places = packed_maps(nx)
    table = jnp.asarray(table)
    x_maps = lax.dynamic_index_in_dim(table, case_of("slab"), keepdims=False)
    y_maps = lax.dynamic_index_in_dim(table, case_of("morton"), keepdims=False)
    pick = lambda maps, i: maps[places[i][0] : places[i][0] + places[i][1], : places[i][2]]
    a1x, a2x = pick(x_maps, 0), pick(x_maps, 1)
    x_one = jnp.einsum("kx,xbyz->kbyz", a1x, one_ext, precision=EXACT)
    x_two = jnp.einsum("kx,xyz->kyz", a2x, two_ext, precision=EXACT)

    narrow = 8
    kx1, kx2 = x_one.shape[0], x_two.shape[0]
    top = jnp.concatenate([flat(x_one[:, :, ny - narrow :]), flat(x_two)])
    bottom = jnp.concatenate([flat(x_one[:, :, :narrow]), flat(x_two)])
    below, above = exchange(bottom, top, "morton")
    split = kx1 * 2 * narrow
    one_ext = jnp.concatenate(
        [
            below[:split].reshape(kx1, 2, narrow, lanes),
            x_one,
            above[:split].reshape(kx1, 2, narrow, lanes),
        ],
        axis=2,
    )
    two_ext = jnp.concatenate(
        [below[split:].reshape(kx2, ny, lanes), x_two, above[split:].reshape(kx2, ny, lanes)],
        axis=1,
    )
    a1y, a2y = pick(y_maps, 2), pick(y_maps, 3)
    y_one = jnp.einsum("ky,abyz->abkz", a1y, one_ext, precision=EXACT)
    y_two = jnp.einsum("ky,ayz->akz", a2y, two_ext, precision=EXACT)

    hx, hy = nx // 2, ny // 2
    level_one = y_one.reshape(2, hx, 2, 2, hy, lanes).transpose(0, 3, 2, 1, 4, 5)
    level_one = level_one.reshape(8, hx, hy, lanes)
    qx, qy, qz = nx // 4, ny // 4, nz // 4
    level_two = y_two.reshape(2, qx, 2, qy, 2, qz).transpose(0, 2, 4, 1, 3, 5)
    level_two = level_two.reshape(8, qx, qy, qz)
    return (level_two[0], level_two[1:], level_one[1:])


def solution(mesh):
    placed = (P("slab", "morton", None),)
    return jax.shard_map(
        per_device,
        mesh=mesh,
        in_specs=placed,
        out_specs=(
            P("slab", "morton", None),
            P(None, "slab", "morton", None),
            P(None, "slab", "morton", None),
        ),
        check_vma=False,
    )
```

```python
import numpy as np
import jax
import jax.numpy as jnp
from jax import lax
from jax.sharding import PartitionSpec as P
from jax.experimental import pallas as pl
from jax.experimental.pallas import tpu as pltpu

LIFT_ALPHA = -1.586134342059924
LIFT_BETA = -0.052980118572961
LIFT_GAMMA = 0.882911075530934
LIFT_DELTA = 0.443506852043971
LIFT_SCALE = 1.149604398860241

EXACT = lax.Precision.HIGHEST


def lift_rows(signal):
    extended = np.pad(signal, ((4, 4), (0, 0)), mode="reflect")
    even, odd = extended[0::2], extended[1::2]
    first_detail = odd[:-1] + LIFT_ALPHA * (even[:-1] + even[1:])
    first_smooth = even[1:-1] + LIFT_BETA * (first_detail[:-1] + first_detail[1:])
    second_detail = first_detail[1:-1] + LIFT_GAMMA * (first_smooth[:-1] + first_smooth[1:])
    second_smooth = first_smooth[1:-1] + LIFT_DELTA * (second_detail[:-1] + second_detail[1:])
    return second_smooth * LIFT_SCALE, second_detail[1:] / LIFT_SCALE


def level_maps(length):
    low, high = lift_rows(np.eye(length))
    low_two, high_two = lift_rows(low)
    return (low, high), (low_two, high_two)


def window_maps(block, halo, level, blocks=8):
    length = block * blocks
    bands = level_maps(length)[level]
    share = block // (2 * (level + 1))
    width = halo[0] + block + halo[1]
    maps = []
    for place in (0, blocks // 2, blocks - 1):
        rows = np.concatenate([band[place * share : (place + 1) * share] for band in bands])
        matrix = np.zeros((rows.shape[0], width))
        for i in range(width):
            cell = place * block - halo[0] + i
            if 0 <= cell < length:
                matrix[:, i] = rows[:, cell]
        maps.append(matrix.astype(np.float32))
    return maps


def packed_maps(block):
    parts = [
        window_maps(block, (4, 4), 0),
        window_maps(block, (12, 12), 1),
        window_maps(block, (8, 8), 0),
        window_maps(block, (block, block), 1),
    ]
    height = sum(p[0].shape[0] for p in parts)
    width = -(-max(p[0].shape[1] for p in parts) // 128) * 128
    table = np.zeros((3, height, width), np.float32)
    places, row = [], 0
    for p in parts:
        rows, cols = p[0].shape
        for case in range(3):
            table[case, row : row + rows, :cols] = p[case]
        places.append((row, rows, cols))
        row += rows
    return table, places


def case_of(axis):
    index = lax.axis_index(axis)
    last = lax.axis_size(axis) - 1
    return jnp.where(index == 0, 0, jnp.where(index == last, 2, 1))


def exchange(lower_half, upper_half, axis):
    devices = lax.axis_size(axis)
    up = [(i, i + 1) for i in range(devices - 1)]
    down = [(i + 1, i) for i in range(devices - 1)]
    from_below = lax.ppermute(upper_half, axis, up)
    from_above = lax.ppermute(lower_half, axis, down)
    return from_below, from_above


def y_pass_kernel(one_ref, two_ref, below_ref, above_ref, a1_ref, a2_ref, approx_ref, two_out, one_out):
    n_two, lanes = two_ref.shape
    n_one = one_ref.shape[0]
    ny = 2 * one_out.shape[2]
    slabs_one = n_one // ny
    slabs_two = n_two // ny
    narrow = (below_ref.shape[0] - n_two) // slabs_one
    blocks = []
    for s in range(slabs_one):
        blocks.append(
            jnp.concatenate(
                [
                    below_ref[s * narrow : (s + 1) * narrow, :],
                    one_ref[s * ny : (s + 1) * ny, :],
                    above_ref[s * narrow : (s + 1) * narrow, :],
                ]
            )
        )
    result = jnp.dot(a1_ref[...], jnp.concatenate(blocks, axis=1), precision=EXACT,
                     preferred_element_type=jnp.float32)
    half_x, half_y = one_out.shape[1], one_out.shape[2]
    for s in range(slabs_one):
        kx, bz = divmod(s, 2)
        bx, kx8 = divmod(kx, half_x)
        block = result[:, s * lanes : (s + 1) * lanes]
        for by in range(2):
            band = 4 * bx + 2 * by + bz
            if band:
                one_out[band - 1, kx8] = block[by * half_y : (by + 1) * half_y]
    base = n_one // ny * narrow
    blocks = []
    for s in range(slabs_two):
        blocks.append(
            jnp.concatenate(
                [
                    below_ref[base + s * ny : base + (s + 1) * ny, :],
                    two_ref[s * ny : (s + 1) * ny, :],
                    above_ref[base + s * ny : base + (s + 1) * ny, :],
                ]
            )
        )
    result = jnp.dot(a2_ref[...], jnp.concatenate(blocks, axis=1), precision=EXACT,
                     preferred_element_type=jnp.float32)
    quarter_x, quarter_y, quarter_z = approx_ref.shape
    for s in range(slabs_two):
        bx, kx4 = divmod(s, quarter_x)
        block = result[:, s * lanes : (s + 1) * lanes]
        for by in range(2):
            for bz in range(2):
                piece = block[by * quarter_y : (by + 1) * quarter_y, bz * quarter_z : (bz + 1) * quarter_z]
                band = 4 * bx + 2 * by + bz
                if band:
                    two_out[band - 1, kx4] = piece
                else:
                    approx_ref[kx4] = piece


def y_pass(x_one, x_two, below, above, a1y, a2y, nx, ny, nz):
    vmem = pl.BlockSpec(memory_space=pltpu.VMEM)
    lanes = x_one.shape[-1]
    return pl.pallas_call(
        y_pass_kernel,
        out_shape=(
            jax.ShapeDtypeStruct((nx // 4, ny // 4, nz // 4), jnp.float32),
            jax.ShapeDtypeStruct((7, nx // 4, ny // 4, nz // 4), jnp.float32),
            jax.ShapeDtypeStruct((7, nx // 2, ny // 2, lanes), jnp.float32),
        ),
        in_specs=[vmem] * 6,
        out_specs=(vmem, vmem, vmem),
    )(x_one.reshape(-1, lanes), x_two.reshape(-1, lanes), below, above, a1y, a2y)


def per_device(velocity):
    nx, ny, nz = velocity.shape

    (z_low, z_high), (z2_low, z2_high) = level_maps(nz)
    z_maps = np.stack([z_low.T, z_high.T, np.concatenate([z2_low, z2_high]).T]).astype(np.float32)
    lanes = z_maps.shape[2]
    u = jnp.einsum("xyz,bzk->xbyk", velocity, jnp.asarray(z_maps), precision=EXACT)

    wide = 12
    one_rows = u[:, 0:2]
    two_rows = u[:, 2]
    flat = lambda a: a.reshape(-1, lanes)
    top = jnp.concatenate([flat(one_rows[nx - 4 :]), flat(two_rows[nx - wide :])])
    bottom = jnp.concatenate([flat(one_rows[:4]), flat(two_rows[:wide])])
    below, above = exchange(bottom, top, "slab")
    split = 4 * 2 * ny
    one_ext = jnp.concatenate(
        [below[:split].reshape(4, 2, ny, lanes), one_rows, above[:split].reshape(4, 2, ny, lanes)]
    )
    two_ext = jnp.concatenate(
        [below[split:].reshape(wide, ny, lanes), two_rows, above[split:].reshape(wide, ny, lanes)]
    )
    assert nx == ny and wide == 12
    table, places = packed_maps(nx)
    table = jnp.asarray(table)
    x_maps = lax.dynamic_index_in_dim(table, case_of("slab"), keepdims=False)
    y_maps = lax.dynamic_index_in_dim(table, case_of("morton"), keepdims=False)
    pick = lambda maps, i: maps[places[i][0] : places[i][0] + places[i][1], : places[i][2]]
    a1x, a2x = pick(x_maps, 0), pick(x_maps, 1)
    x_one = jnp.einsum("kx,xbyz->kbyz", a1x, one_ext, precision=EXACT)
    x_two = jnp.einsum("kx,xyz->kyz", a2x, two_ext, precision=EXACT)

    narrow = 8
    kx1, kx2 = x_one.shape[0], x_two.shape[0]
    top = jnp.concatenate([flat(x_one[:, :, ny - narrow :]), flat(x_two)])
    bottom = jnp.concatenate([flat(x_one[:, :, :narrow]), flat(x_two)])
    below, above = exchange(bottom, top, "morton")
    a1y, a2y = pick(y_maps, 2), pick(y_maps, 3)
    return y_pass(x_one, x_two, below, above, a1y, a2y, nx, ny, nz)


def solution(mesh):
    placed = (P("slab", "morton", None),)
    return jax.shard_map(
        per_device,
        mesh=mesh,
        in_specs=placed,
        out_specs=(
            P("slab", "morton", None),
            P(None, "slab", "morton", None),
            P(None, "slab", "morton", None),
        ),
        check_vma=False,
    )
```

```python
import functools

import numpy as np
import jax
import jax.numpy as jnp
from jax import lax
from jax.sharding import PartitionSpec as P
from jax.experimental import pallas as pl
from jax.experimental.pallas import tpu as pltpu

LIFT_ALPHA = -1.586134342059924
LIFT_BETA = -0.052980118572961
LIFT_GAMMA = 0.882911075530934
LIFT_DELTA = 0.443506852043971
LIFT_SCALE = 1.149604398860241

EXACT = lax.Precision.HIGHEST


def lift_rows(signal):
    extended = np.pad(signal, ((4, 4), (0, 0)), mode="reflect")
    even, odd = extended[0::2], extended[1::2]
    first_detail = odd[:-1] + LIFT_ALPHA * (even[:-1] + even[1:])
    first_smooth = even[1:-1] + LIFT_BETA * (first_detail[:-1] + first_detail[1:])
    second_detail = first_detail[1:-1] + LIFT_GAMMA * (first_smooth[:-1] + first_smooth[1:])
    second_smooth = first_smooth[1:-1] + LIFT_DELTA * (second_detail[:-1] + second_detail[1:])
    return second_smooth * LIFT_SCALE, second_detail[1:] / LIFT_SCALE


def level_maps(length):
    low, high = lift_rows(np.eye(length))
    low_two, high_two = lift_rows(low)
    return (low, high), (low_two, high_two)


def window_maps(block, halo, level, blocks=8):
    length = block * blocks
    bands = level_maps(length)[level]
    share = block // (2 * (level + 1))
    width = halo[0] + block + halo[1]
    maps = []
    for place in (0, blocks // 2, blocks - 1):
        rows = np.concatenate([band[place * share : (place + 1) * share] for band in bands])
        matrix = np.zeros((rows.shape[0], width))
        for i in range(width):
            cell = place * block - halo[0] + i
            if 0 <= cell < length:
                matrix[:, i] = rows[:, cell]
        maps.append(matrix.astype(np.float32))
    return maps


def packed_maps(block):
    parts = [
        window_maps(block, (4, 4), 0),
        window_maps(block, (12, 12), 1),
        window_maps(block, (8, 8), 0),
        window_maps(block, (block, block), 1),
    ]
    height = sum(p[0].shape[0] for p in parts)
    width = -(-max(p[0].shape[1] for p in parts) // 128) * 128
    table = np.zeros((3, height, width), np.float32)
    places, row = [], 0
    for p in parts:
        rows, cols = p[0].shape
        for case in range(3):
            table[case, row : row + rows, :cols] = p[case]
        places.append((row, rows, cols))
        row += rows
    return table, places


def case_of(axis):
    index = lax.axis_index(axis)
    last = lax.axis_size(axis) - 1
    return jnp.where(index == 0, 0, jnp.where(index == last, 2, 1))


def exchange(lower_half, upper_half, axis):
    devices = lax.axis_size(axis)
    up = [(i, i + 1) for i in range(devices - 1)]
    down = [(i + 1, i) for i in range(devices - 1)]
    from_below = lax.ppermute(upper_half, axis, up)
    from_above = lax.ppermute(lower_half, axis, down)
    return from_below, from_above


def y_pass_kernel(one_ref, two_ref, below_ref, above_ref, maps_ref, approx_ref, two_out, one_out, *, places):
    n_two, lanes = two_ref.shape
    n_one = one_ref.shape[0]
    ny = 2 * one_out.shape[2]
    slabs_one = n_one // ny
    slabs_two = n_two // ny
    narrow = (below_ref.shape[0] - n_two) // slabs_one
    blocks = []
    for s in range(slabs_one):
        blocks.append(
            jnp.concatenate(
                [
                    below_ref[s * narrow : (s + 1) * narrow, :],
                    one_ref[s * ny : (s + 1) * ny, :],
                    above_ref[s * narrow : (s + 1) * narrow, :],
                ]
            )
        )
    row, rows, cols = places[2]
    a1 = maps_ref[row : row + rows, :][:, :cols]
    result = jnp.dot(a1, jnp.concatenate(blocks, axis=1), precision=EXACT,
                     preferred_element_type=jnp.float32)
    half_x, half_y = one_out.shape[1], one_out.shape[2]
    for s in range(slabs_one):
        kx, bz = divmod(s, 2)
        bx, kx8 = divmod(kx, half_x)
        block = result[:, s * lanes : (s + 1) * lanes]
        for by in range(2):
            band = 4 * bx + 2 * by + bz
            if band:
                one_out[band - 1, kx8] = block[by * half_y : (by + 1) * half_y]
    base = n_one // ny * narrow
    blocks = []
    for s in range(slabs_two):
        blocks.append(
            jnp.concatenate(
                [
                    below_ref[base + s * ny : base + (s + 1) * ny, :],
                    two_ref[s * ny : (s + 1) * ny, :],
                    above_ref[base + s * ny : base + (s + 1) * ny, :],
                ]
            )
        )
    row, rows, cols = places[3]
    a2 = maps_ref[row : row + rows, :][:, :cols]
    result = jnp.dot(a2, jnp.concatenate(blocks, axis=1), precision=EXACT,
                     preferred_element_type=jnp.float32)
    quarter_x, quarter_y, quarter_z = approx_ref.shape
    for s in range(slabs_two):
        bx, kx4 = divmod(s, quarter_x)
        block = result[:, s * lanes : (s + 1) * lanes]
        for by in range(2):
            for bz in range(2):
                piece = block[by * quarter_y : (by + 1) * quarter_y, bz * quarter_z : (bz + 1) * quarter_z]
                band = 4 * bx + 2 * by + bz
                if band:
                    two_out[band - 1, kx4] = piece
                else:
                    approx_ref[kx4] = piece


def y_pass(x_one, x_two, below, above, y_maps, places, nx, ny, nz):
    vmem = pl.BlockSpec(memory_space=pltpu.VMEM)
    lanes = x_one.shape[-1]
    return pl.pallas_call(
        functools.partial(y_pass_kernel, places=tuple(places)),
        out_shape=(
            jax.ShapeDtypeStruct((nx // 4, ny // 4, nz // 4), jnp.float32),
            jax.ShapeDtypeStruct((7, nx // 4, ny // 4, nz // 4), jnp.float32),
            jax.ShapeDtypeStruct((7, nx // 2, ny // 2, lanes), jnp.float32),
        ),
        in_specs=[vmem] * 5,
        out_specs=(vmem, vmem, vmem),
    )(x_one.reshape(-1, lanes), x_two.reshape(-1, lanes), below, above, y_maps)


def per_device(velocity):
    nx, ny, nz = velocity.shape

    (z_low, z_high), (z2_low, z2_high) = level_maps(nz)
    z_maps = np.stack([z_low.T, z_high.T, np.concatenate([z2_low, z2_high]).T]).astype(np.float32)
    lanes = z_maps.shape[2]
    u = jnp.einsum("xyz,bzk->xbyk", velocity, jnp.asarray(z_maps), precision=EXACT)

    wide = 12
    one_rows = u[:, 0:2]
    two_rows = u[:, 2]
    flat = lambda a: a.reshape(-1, lanes)
    top = jnp.concatenate([flat(one_rows[nx - 4 :]), flat(two_rows[nx - wide :])])
    bottom = jnp.concatenate([flat(one_rows[:4]), flat(two_rows[:wide])])
    below, above = exchange(bottom, top, "slab")
    split = 4 * 2 * ny
    one_ext = jnp.concatenate(
        [below[:split].reshape(4, 2, ny, lanes), one_rows, above[:split].reshape(4, 2, ny, lanes)]
    )
    two_ext = jnp.concatenate(
        [below[split:].reshape(wide, ny, lanes), two_rows, above[split:].reshape(wide, ny, lanes)]
    )
    assert nx == ny and wide == 12
    table, places = packed_maps(nx)
    table = jnp.asarray(table)
    x_maps = lax.dynamic_index_in_dim(table, case_of("slab"), keepdims=False)
    y_maps = lax.dynamic_index_in_dim(table, case_of("morton"), keepdims=False)
    pick = lambda maps, i: maps[places[i][0] : places[i][0] + places[i][1], : places[i][2]]
    a1x, a2x = pick(x_maps, 0), pick(x_maps, 1)
    x_one = jnp.einsum("kx,xbyz->kbyz", a1x, one_ext, precision=EXACT)
    x_two = jnp.einsum("kx,xyz->kyz", a2x, two_ext, precision=EXACT)

    narrow = 8
    kx1, kx2 = x_one.shape[0], x_two.shape[0]
    top = jnp.concatenate([flat(x_one[:, :, ny - narrow :]), flat(x_two)])
    bottom = jnp.concatenate([flat(x_one[:, :, :narrow]), flat(x_two)])
    below, above = exchange(bottom, top, "morton")
    return y_pass(x_one, x_two, below, above, y_maps, places, nx, ny, nz)


def solution(mesh):
    placed = (P("slab", "morton", None),)
    return jax.shard_map(
        per_device,
        mesh=mesh,
        in_specs=placed,
        out_specs=(
            P("slab", "morton", None),
            P(None, "slab", "morton", None),
            P(None, "slab", "morton", None),
        ),
        check_vma=False,
    )
```

```python
import functools

import numpy as np
import jax
import jax.numpy as jnp
from jax import lax
from jax.sharding import PartitionSpec as P
from jax.experimental import pallas as pl
from jax.experimental.pallas import tpu as pltpu

LIFT_ALPHA = -1.586134342059924
LIFT_BETA = -0.052980118572961
LIFT_GAMMA = 0.882911075530934
LIFT_DELTA = 0.443506852043971
LIFT_SCALE = 1.149604398860241

EXACT = lax.Precision.HIGHEST


def lift_rows(signal):
    extended = np.pad(signal, ((4, 4), (0, 0)), mode="reflect")
    even, odd = extended[0::2], extended[1::2]
    first_detail = odd[:-1] + LIFT_ALPHA * (even[:-1] + even[1:])
    first_smooth = even[1:-1] + LIFT_BETA * (first_detail[:-1] + first_detail[1:])
    second_detail = first_detail[1:-1] + LIFT_GAMMA * (first_smooth[:-1] + first_smooth[1:])
    second_smooth = first_smooth[1:-1] + LIFT_DELTA * (second_detail[:-1] + second_detail[1:])
    return second_smooth * LIFT_SCALE, second_detail[1:] / LIFT_SCALE


def level_maps(length):
    low, high = lift_rows(np.eye(length))
    low_two, high_two = lift_rows(low)
    return (low, high), (low_two, high_two)


def window_maps(block, halo, level, blocks=8):
    length = block * blocks
    bands = level_maps(length)[level]
    share = block // (2 * (level + 1))
    width = halo[0] + block + halo[1]
    maps = []
    for place in (0, blocks // 2, blocks - 1):
        rows = np.concatenate([band[place * share : (place + 1) * share] for band in bands])
        matrix = np.zeros((rows.shape[0], width))
        for i in range(width):
            cell = place * block - halo[0] + i
            if 0 <= cell < length:
                matrix[:, i] = rows[:, cell]
        maps.append(matrix.astype(np.float32))
    return maps


def packed_maps(block):
    parts = [
        window_maps(block, (4, 4), 0),
        window_maps(block, (12, 12), 1),
        window_maps(block, (8, 8), 0),
        window_maps(block, (block, block), 1),
    ]
    height = sum(p[0].shape[0] for p in parts)
    width = -(-max(p[0].shape[1] for p in parts) // 128) * 128
    table = np.zeros((3, height, width), np.float32)
    places, row = [], 0
    for p in parts:
        rows, cols = p[0].shape
        for case in range(3):
            table[case, row : row + rows, :cols] = p[case]
        places.append((row, rows, cols))
        row += rows
    return table, places


def case_of(axis):
    index = lax.axis_index(axis)
    last = lax.axis_size(axis) - 1
    return jnp.where(index == 0, 0, jnp.where(index == last, 2, 1))


def exchange(lower_half, upper_half, axis):
    devices = lax.axis_size(axis)
    up = [(i, i + 1) for i in range(devices - 1)]
    down = [(i + 1, i) for i in range(devices - 1)]
    from_below = lax.ppermute(upper_half, axis, up)
    from_above = lax.ppermute(lower_half, axis, down)
    return from_below, from_above


def y_pass_kernel(one_ref, two_ref, below_ref, above_ref, maps_ref, approx_ref, two_out, one_out, *, places):
    n_two, lanes = two_ref.shape
    n_one = one_ref.shape[0]
    ny = 2 * one_out.shape[2]
    slabs_one = n_one // ny
    slabs_two = n_two // ny
    narrow = (below_ref.shape[0] - n_two) // slabs_one
    blocks = []
    for s in range(slabs_one):
        blocks.append(
            jnp.concatenate(
                [
                    below_ref[s * narrow : (s + 1) * narrow, :],
                    one_ref[s * ny : (s + 1) * ny, :],
                    above_ref[s * narrow : (s + 1) * narrow, :],
                ]
            )
        )
    row, rows, cols = places[2]
    a1 = maps_ref[row : row + rows, :][:, :cols]
    result = jnp.dot(a1, jnp.concatenate(blocks, axis=1), precision=EXACT,
                     preferred_element_type=jnp.float32)
    half_x, half_y = one_out.shape[1], one_out.shape[2]
    for s in range(slabs_one):
        kx, bz = divmod(s, 2)
        bx, kx8 = divmod(kx, half_x)
        block = result[:, s * lanes : (s + 1) * lanes]
        for by in range(2):
            band = 4 * bx + 2 * by + bz
            if band:
                one_out[band - 1, kx8] = block[by * half_y : (by + 1) * half_y]
    base = n_one // ny * narrow
    blocks = []
    for s in range(slabs_two):
        blocks.append(
            jnp.concatenate(
                [
                    below_ref[base + s * ny : base + (s + 1) * ny, :],
                    two_ref[s * ny : (s + 1) * ny, :],
                    above_ref[base + s * ny : base + (s + 1) * ny, :],
                ]
            )
        )
    row, rows, cols = places[3]
    a2 = maps_ref[row : row + rows, :][:, :cols]
    result = jnp.dot(a2, jnp.concatenate(blocks, axis=1), precision=EXACT,
                     preferred_element_type=jnp.float32)
    quarter_x, quarter_y, quarter_z = approx_ref.shape
    for s in range(slabs_two):
        bx, kx4 = divmod(s, quarter_x)
        block = result[:, s * lanes : (s + 1) * lanes]
        for by in range(2):
            for bz in range(2):
                piece = block[by * quarter_y : (by + 1) * quarter_y, bz * quarter_z : (bz + 1) * quarter_z]
                band = 4 * bx + 2 * by + bz
                if band:
                    two_out[band - 1, kx4] = piece
                else:
                    approx_ref[kx4] = piece


def y_pass(x_one, x_two, below, above, y_maps, places, nx, ny, nz):
    vmem = pl.BlockSpec(memory_space=pltpu.VMEM)
    lanes = x_one.shape[-1]
    return pl.pallas_call(
        functools.partial(y_pass_kernel, places=tuple(places)),
        out_shape=(
            jax.ShapeDtypeStruct((nx // 4, ny // 4, nz // 4), jnp.float32),
            jax.ShapeDtypeStruct((7, nx // 4, ny // 4, nz // 4), jnp.float32),
            jax.ShapeDtypeStruct((7, nx // 2, ny // 2, lanes), jnp.float32),
        ),
        in_specs=[vmem] * 5,
        out_specs=(vmem, vmem, vmem),
    )(x_one.reshape(-1, lanes), x_two.reshape(-1, lanes), below, above, y_maps)


def x_pass_kernel(own_ref, below_ref, above_ref, maps_ref, one_out, two_out, top_out, bottom_out, *,
                  taps, places, bands):
    ny = two_out.shape[0] // len(taps[1])
    slab = 2 * ny
    stride = bands * ny
    lo1, lo2 = 4, 12
    split = lo1 * slab

    def one_slab(i):
        if i < lo1:
            return below_ref[i * slab : (i + 1) * slab, :]
        if i < lo1 + ny:
            return own_ref[(i - lo1) * stride : (i - lo1) * stride + slab, :]
        j = i - lo1 - ny
        return above_ref[j * slab : (j + 1) * slab, :]

    def two_slab(i):
        if i < lo2:
            return below_ref[split + i * ny : split + (i + 1) * ny, :]
        if i < lo2 + ny:
            at = (i - lo2) * stride + slab
            return own_ref[at : at + ny, :]
        j = i - lo2 - ny
        return above_ref[split + j * ny : split + (j + 1) * ny, :]

    narrow = (top_out.shape[0] - two_out.shape[0]) // (len(taps[0]) * 2)
    row1 = places[0][0]
    for k, used in enumerate(taps[0]):
        acc = None
        for i in used:
            term = maps_ref[row1 + k, i] * one_slab(i)
            acc = term if acc is None else acc + term
        one_out[k * slab : (k + 1) * slab, :] = acc
        for b in range(2):
            at = (k * 2 + b) * narrow
            top_out[at : at + narrow, :] = acc[b * ny + ny - narrow : (b + 1) * ny, :]
            bottom_out[at : at + narrow, :] = acc[b * ny : b * ny + narrow, :]
    base = len(taps[0]) * 2 * narrow
    row2 = places[1][0]
    for k, used in enumerate(taps[1]):
        acc = None
        for i in used:
            term = maps_ref[row2 + k, i] * two_slab(i)
            acc = term if acc is None else acc + term
        two_out[k * ny : (k + 1) * ny, :] = acc
        top_out[base + k * ny : base + (k + 1) * ny, :] = acc
        bottom_out[base + k * ny : base + (k + 1) * ny, :] = acc


def used_taps(maps):
    present = np.any(np.stack([m != 0 for m in maps]), axis=0)
    return tuple(tuple(int(i) for i in np.nonzero(row)[0]) for row in present)


def x_pass(u, below, above, x_maps, places, nx, ny):
    lanes = u.shape[-1]
    taps = (used_taps(window_maps(nx, (4, 4), 0)), used_taps(window_maps(nx, (12, 12), 1)))
    narrow = 8
    vmem = pl.BlockSpec(memory_space=pltpu.VMEM)
    smem = pl.BlockSpec(memory_space=pltpu.SMEM)
    message = len(taps[0]) * 2 * narrow + len(taps[1]) * ny
    return pl.pallas_call(
        functools.partial(x_pass_kernel, taps=taps, places=tuple(places), bands=u.shape[1]),
        out_shape=(
            jax.ShapeDtypeStruct((len(taps[0]) * 2 * ny, lanes), jnp.float32),
            jax.ShapeDtypeStruct((len(taps[1]) * ny, lanes), jnp.float32),
            jax.ShapeDtypeStruct((message, lanes), jnp.float32),
            jax.ShapeDtypeStruct((message, lanes), jnp.float32),
        ),
        in_specs=[vmem, vmem, vmem, smem],
        out_specs=(vmem, vmem, vmem, vmem),
    )(u.reshape(-1, lanes), below, above, x_maps)


def per_device(velocity):
    nx, ny, nz = velocity.shape

    (z_low, z_high), (z2_low, z2_high) = level_maps(nz)
    z_maps = np.stack([z_low.T, z_high.T, np.concatenate([z2_low, z2_high]).T]).astype(np.float32)
    lanes = z_maps.shape[2]
    u = jnp.einsum("xyz,bzk->xbyk", velocity, jnp.asarray(z_maps), precision=EXACT)

    wide = 12
    one_rows = u[:, 0:2]
    two_rows = u[:, 2]
    flat = lambda a: a.reshape(-1, lanes)
    top = jnp.concatenate([flat(one_rows[nx - 4 :]), flat(two_rows[nx - wide :])])
    bottom = jnp.concatenate([flat(one_rows[:4]), flat(two_rows[:wide])])
    below, above = exchange(bottom, top, "slab")
    assert nx == ny and wide == 12
    table, places = packed_maps(nx)
    table = jnp.asarray(table)
    x_maps = lax.dynamic_index_in_dim(table, case_of("slab"), keepdims=False)
    y_maps = lax.dynamic_index_in_dim(table, case_of("morton"), keepdims=False)
    x_one, x_two, top, bottom = x_pass(u, below, above, x_maps, places, nx, ny)

    below, above = exchange(bottom, top, "morton")
    return y_pass(x_one, x_two, below, above, y_maps, places, nx, ny, nz)


def solution(mesh):
    placed = (P("slab", "morton", None),)
    return jax.shard_map(
        per_device,
        mesh=mesh,
        in_specs=placed,
        out_specs=(
            P("slab", "morton", None),
            P(None, "slab", "morton", None),
            P(None, "slab", "morton", None),
        ),
        check_vma=False,
    )
```

```python
import functools

import numpy as np
import jax
import jax.numpy as jnp
from jax import lax
from jax.sharding import PartitionSpec as P
from jax.experimental import pallas as pl
from jax.experimental.pallas import tpu as pltpu

LIFT_ALPHA = -1.586134342059924
LIFT_BETA = -0.052980118572961
LIFT_GAMMA = 0.882911075530934
LIFT_DELTA = 0.443506852043971
LIFT_SCALE = 1.149604398860241

EXACT = lax.Precision.HIGHEST


def lift_rows(signal):
    extended = np.pad(signal, ((4, 4), (0, 0)), mode="reflect")
    even, odd = extended[0::2], extended[1::2]
    first_detail = odd[:-1] + LIFT_ALPHA * (even[:-1] + even[1:])
    first_smooth = even[1:-1] + LIFT_BETA * (first_detail[:-1] + first_detail[1:])
    second_detail = first_detail[1:-1] + LIFT_GAMMA * (first_smooth[:-1] + first_smooth[1:])
    second_smooth = first_smooth[1:-1] + LIFT_DELTA * (second_detail[:-1] + second_detail[1:])
    return second_smooth * LIFT_SCALE, second_detail[1:] / LIFT_SCALE


def level_maps(length):
    low, high = lift_rows(np.eye(length))
    low_two, high_two = lift_rows(low)
    return (low, high), (low_two, high_two)


def window_maps(block, halo, level, blocks=8):
    length = block * blocks
    bands = level_maps(length)[level]
    share = block // (2 * (level + 1))
    width = halo[0] + block + halo[1]
    maps = []
    for place in (0, blocks // 2, blocks - 1):
        rows = np.concatenate([band[place * share : (place + 1) * share] for band in bands])
        matrix = np.zeros((rows.shape[0], width))
        for i in range(width):
            cell = place * block - halo[0] + i
            if 0 <= cell < length:
                matrix[:, i] = rows[:, cell]
        maps.append(matrix.astype(np.float32))
    return maps


def packed_maps(block):
    parts = [
        window_maps(block, (4, 4), 0),
        window_maps(block, (12, 12), 1),
        window_maps(block, (8, 8), 0),
        window_maps(block, (block, block), 1),
    ]
    height = sum(p[0].shape[0] for p in parts)
    width = -(-max(p[0].shape[1] for p in parts) // 128) * 128
    table = np.zeros((3, height, width), np.float32)
    places, row = [], 0
    for p in parts:
        rows, cols = p[0].shape
        for case in range(3):
            table[case, row : row + rows, :cols] = p[case]
        places.append((row, rows, cols))
        row += rows
    return table, places


def case_of(axis):
    index = lax.axis_index(axis)
    last = lax.axis_size(axis) - 1
    return jnp.where(index == 0, 0, jnp.where(index == last, 2, 1))


def exchange(lower_half, upper_half, axis):
    devices = lax.axis_size(axis)
    up = [(i, i + 1) for i in range(devices - 1)]
    down = [(i + 1, i) for i in range(devices - 1)]
    from_below = lax.ppermute(upper_half, axis, up)
    from_above = lax.ppermute(lower_half, axis, down)
    return from_below, from_above


def y_pass_kernel(one_ref, two_ref, below_ref, above_ref, maps_ref, approx_ref, two_out, one_out, *, places):
    n_two, lanes = two_ref.shape
    n_one = one_ref.shape[0]
    ny = 2 * one_out.shape[2]
    slabs_one = n_one // ny
    slabs_two = n_two // ny
    narrow = (below_ref.shape[0] - n_two) // slabs_one
    blocks = []
    for s in range(slabs_one):
        blocks.append(
            jnp.concatenate(
                [
                    below_ref[s * narrow : (s + 1) * narrow, :],
                    one_ref[s * ny : (s + 1) * ny, :],
                    above_ref[s * narrow : (s + 1) * narrow, :],
                ]
            )
        )
    row, rows, cols = places[2]
    a1 = maps_ref[row : row + rows, :][:, :cols]
    result = jnp.dot(a1, jnp.concatenate(blocks, axis=1), precision=EXACT,
                     preferred_element_type=jnp.float32)
    half_x, half_y = one_out.shape[1], one_out.shape[2]
    for s in range(slabs_one):
        kx, bz = divmod(s, 2)
        bx, kx8 = divmod(kx, half_x)
        block = result[:, s * lanes : (s + 1) * lanes]
        for by in range(2):
            band = 4 * bx + 2 * by + bz
            if band:
                one_out[band - 1, kx8] = block[by * half_y : (by + 1) * half_y]
    base = n_one // ny * narrow
    blocks = []
    for s in range(slabs_two):
        blocks.append(
            jnp.concatenate(
                [
                    below_ref[base + s * ny : base + (s + 1) * ny, :],
                    two_ref[s * ny : (s + 1) * ny, :],
                    above_ref[base + s * ny : base + (s + 1) * ny, :],
                ]
            )
        )
    row, rows, cols = places[3]
    a2 = maps_ref[row : row + rows, :][:, :cols]
    result = jnp.dot(a2, jnp.concatenate(blocks, axis=1), precision=EXACT,
                     preferred_element_type=jnp.float32)
    quarter_x, quarter_y, quarter_z = approx_ref.shape
    for s in range(slabs_two):
        bx, kx4 = divmod(s, quarter_x)
        block = result[:, s * lanes : (s + 1) * lanes]
        for by in range(2):
            for bz in range(2):
                piece = block[by * quarter_y : (by + 1) * quarter_y, bz * quarter_z : (bz + 1) * quarter_z]
                band = 4 * bx + 2 * by + bz
                if band:
                    two_out[band - 1, kx4] = piece
                else:
                    approx_ref[kx4] = piece


def y_pass(x_one, x_two, below, above, y_maps, places, nx, ny, nz):
    vmem = pl.BlockSpec(memory_space=pltpu.VMEM)
    lanes = x_one.shape[-1]
    return pl.pallas_call(
        functools.partial(y_pass_kernel, places=tuple(places)),
        out_shape=(
            jax.ShapeDtypeStruct((nx // 4, ny // 4, nz // 4), jnp.float32),
            jax.ShapeDtypeStruct((7, nx // 4, ny // 4, nz // 4), jnp.float32),
            jax.ShapeDtypeStruct((7, nx // 2, ny // 2, lanes), jnp.float32),
        ),
        in_specs=[vmem] * 5,
        out_specs=(vmem, vmem, vmem),
    )(x_one.reshape(-1, lanes), x_two.reshape(-1, lanes), below, above, y_maps)


def x_pass_kernel(own_ref, below_ref, above_ref, maps_ref, one_out, two_out, top_out, bottom_out, *,
                  taps, places, bands):
    ny = two_out.shape[0] // len(taps[1])
    slab = 2 * ny
    plane = own_ref.shape[0] // bands
    lo1, lo2 = 4, 12
    split = lo1 * slab

    def one_slab(i):
        if i < lo1:
            return below_ref[i * slab : (i + 1) * slab, :]
        if i < lo1 + ny:
            at = (i - lo1) * ny
            return jnp.concatenate([own_ref[at : at + ny, :], own_ref[plane + at : plane + at + ny, :]])
        j = i - lo1 - ny
        return above_ref[j * slab : (j + 1) * slab, :]

    def two_slab(i):
        if i < lo2:
            return below_ref[split + i * ny : split + (i + 1) * ny, :]
        if i < lo2 + ny:
            at = 2 * plane + (i - lo2) * ny
            return own_ref[at : at + ny, :]
        j = i - lo2 - ny
        return above_ref[split + j * ny : split + (j + 1) * ny, :]

    narrow = (top_out.shape[0] - two_out.shape[0]) // (len(taps[0]) * 2)
    row1 = places[0][0]
    for k, used in enumerate(taps[0]):
        acc = None
        for i in used:
            term = maps_ref[row1 + k, i] * one_slab(i)
            acc = term if acc is None else acc + term
        one_out[k * slab : (k + 1) * slab, :] = acc
        for b in range(2):
            at = (k * 2 + b) * narrow
            top_out[at : at + narrow, :] = acc[b * ny + ny - narrow : (b + 1) * ny, :]
            bottom_out[at : at + narrow, :] = acc[b * ny : b * ny + narrow, :]
    base = len(taps[0]) * 2 * narrow
    row2 = places[1][0]
    for k, used in enumerate(taps[1]):
        acc = None
        for i in used:
            term = maps_ref[row2 + k, i] * two_slab(i)
            acc = term if acc is None else acc + term
        two_out[k * ny : (k + 1) * ny, :] = acc
        top_out[base + k * ny : base + (k + 1) * ny, :] = acc
        bottom_out[base + k * ny : base + (k + 1) * ny, :] = acc


def used_taps(maps):
    present = np.any(np.stack([m != 0 for m in maps]), axis=0)
    return tuple(tuple(int(i) for i in np.nonzero(row)[0]) for row in present)


def x_pass(u, below, above, x_maps, places, nx, ny):
    lanes = u.shape[-1]
    taps = (used_taps(window_maps(nx, (4, 4), 0)), used_taps(window_maps(nx, (12, 12), 1)))
    narrow = 8
    vmem = pl.BlockSpec(memory_space=pltpu.VMEM)
    smem = pl.BlockSpec(memory_space=pltpu.SMEM)
    message = len(taps[0]) * 2 * narrow + len(taps[1]) * ny
    return pl.pallas_call(
        functools.partial(x_pass_kernel, taps=taps, places=tuple(places), bands=u.shape[1]),
        out_shape=(
            jax.ShapeDtypeStruct((len(taps[0]) * 2 * ny, lanes), jnp.float32),
            jax.ShapeDtypeStruct((len(taps[1]) * ny, lanes), jnp.float32),
            jax.ShapeDtypeStruct((message, lanes), jnp.float32),
            jax.ShapeDtypeStruct((message, lanes), jnp.float32),
        ),
        in_specs=[vmem, vmem, vmem, smem],
        out_specs=(vmem, vmem, vmem, vmem),
    )(u.transpose(1, 0, 2, 3).reshape(-1, lanes), below, above, x_maps)


def per_device(velocity):
    nx, ny, nz = velocity.shape

    (z_low, z_high), (z2_low, z2_high) = level_maps(nz)
    z_maps = np.stack([z_low.T, z_high.T, np.concatenate([z2_low, z2_high]).T]).astype(np.float32)
    lanes = z_maps.shape[2]
    u = jnp.einsum("xyz,bzk->xbyk", velocity, jnp.asarray(z_maps), precision=EXACT)

    wide = 12
    one_rows = u[:, 0:2]
    two_rows = u[:, 2]
    flat = lambda a: a.reshape(-1, lanes)
    top = jnp.concatenate([flat(one_rows[nx - 4 :]), flat(two_rows[nx - wide :])])
    bottom = jnp.concatenate([flat(one_rows[:4]), flat(two_rows[:wide])])
    below, above = exchange(bottom, top, "slab")
    assert nx == ny and wide == 12
    table, places = packed_maps(nx)
    table = jnp.asarray(table)
    x_maps = lax.dynamic_index_in_dim(table, case_of("slab"), keepdims=False)
    y_maps = lax.dynamic_index_in_dim(table, case_of("morton"), keepdims=False)
    x_one, x_two, top, bottom = x_pass(u, below, above, x_maps, places, nx, ny)

    below, above = exchange(bottom, top, "morton")
    return y_pass(x_one, x_two, below, above, y_maps, places, nx, ny, nz)


def solution(mesh):
    placed = (P("slab", "morton", None),)
    return jax.shard_map(
        per_device,
        mesh=mesh,
        in_specs=placed,
        out_specs=(
            P("slab", "morton", None),
            P(None, "slab", "morton", None),
            P(None, "slab", "morton", None),
        ),
        check_vma=False,
    )
```

```python
import functools

import numpy as np
import jax
import jax.numpy as jnp
from jax import lax
from jax.sharding import PartitionSpec as P
from jax.experimental import pallas as pl
from jax.experimental.pallas import tpu as pltpu

LIFT_ALPHA = -1.586134342059924
LIFT_BETA = -0.052980118572961
LIFT_GAMMA = 0.882911075530934
LIFT_DELTA = 0.443506852043971
LIFT_SCALE = 1.149604398860241

EXACT = lax.Precision.HIGHEST


def lift_rows(signal):
    extended = np.pad(signal, ((4, 4), (0, 0)), mode="reflect")
    even, odd = extended[0::2], extended[1::2]
    first_detail = odd[:-1] + LIFT_ALPHA * (even[:-1] + even[1:])
    first_smooth = even[1:-1] + LIFT_BETA * (first_detail[:-1] + first_detail[1:])
    second_detail = first_detail[1:-1] + LIFT_GAMMA * (first_smooth[:-1] + first_smooth[1:])
    second_smooth = first_smooth[1:-1] + LIFT_DELTA * (second_detail[:-1] + second_detail[1:])
    return second_smooth * LIFT_SCALE, second_detail[1:] / LIFT_SCALE


def level_maps(length):
    low, high = lift_rows(np.eye(length))
    low_two, high_two = lift_rows(low)
    return (low, high), (low_two, high_two)


def window_maps(block, halo, level, blocks=8):
    length = block * blocks
    bands = level_maps(length)[level]
    share = block // (2 * (level + 1))
    width = halo[0] + block + halo[1]
    maps = []
    for place in (0, blocks // 2, blocks - 1):
        rows = np.concatenate([band[place * share : (place + 1) * share] for band in bands])
        matrix = np.zeros((rows.shape[0], width))
        for i in range(width):
            cell = place * block - halo[0] + i
            if 0 <= cell < length:
                matrix[:, i] = rows[:, cell]
        maps.append(matrix.astype(np.float32))
    return maps


def packed_maps(block):
    parts = [
        window_maps(block, (4, 4), 0),
        window_maps(block, (12, 12), 1),
        window_maps(block, (8, 8), 0),
        window_maps(block, (block, block), 1),
    ]
    height = sum(p[0].shape[0] for p in parts)
    width = -(-max(p[0].shape[1] for p in parts) // 128) * 128
    table = np.zeros((3, height, width), np.float32)
    places, row = [], 0
    for p in parts:
        rows, cols = p[0].shape
        for case in range(3):
            table[case, row : row + rows, :cols] = p[case]
        places.append((row, rows, cols))
        row += rows
    return table, places


def case_of(axis):
    index = lax.axis_index(axis)
    last = lax.axis_size(axis) - 1
    return jnp.where(index == 0, 0, jnp.where(index == last, 2, 1))


def exchange(lower_half, upper_half, axis):
    devices = lax.axis_size(axis)
    up = [(i, i + 1) for i in range(devices - 1)]
    down = [(i + 1, i) for i in range(devices - 1)]
    from_below = lax.ppermute(upper_half, axis, up)
    from_above = lax.ppermute(lower_half, axis, down)
    return from_below, from_above


def y_pass_kernel(one_ref, two_ref, below_ref, above_ref, maps_ref, approx_ref, two_out, one_out, *, places):
    n_two, lanes = two_ref.shape
    n_one = one_ref.shape[0]
    ny = 2 * one_out.shape[2]
    slabs_one = n_one // ny
    slabs_two = n_two // ny
    narrow = (below_ref.shape[0] - n_two) // slabs_one
    blocks = []
    for s in range(slabs_one):
        blocks.append(
            jnp.concatenate(
                [
                    below_ref[s * narrow : (s + 1) * narrow, :],
                    one_ref[s * ny : (s + 1) * ny, :],
                    above_ref[s * narrow : (s + 1) * narrow, :],
                ]
            )
        )
    row, rows, cols = places[2]
    a1 = maps_ref[row : row + rows, :][:, :cols]
    result = jnp.dot(a1, jnp.concatenate(blocks, axis=1), precision=EXACT,
                     preferred_element_type=jnp.float32)
    half_x, half_y = one_out.shape[1], one_out.shape[2]
    for s in range(slabs_one):
        kx, bz = divmod(s, 2)
        bx, kx8 = divmod(kx, half_x)
        block = result[:, s * lanes : (s + 1) * lanes]
        for by in range(2):
            band = 4 * bx + 2 * by + bz
            if band:
                one_out[band - 1, kx8] = block[by * half_y : (by + 1) * half_y]
    base = n_one // ny * narrow
    blocks = []
    for s in range(slabs_two):
        blocks.append(
            jnp.concatenate(
                [
                    below_ref[base + s * ny : base + (s + 1) * ny, :],
                    two_ref[s * ny : (s + 1) * ny, :],
                    above_ref[base + s * ny : base + (s + 1) * ny, :],
                ]
            )
        )
    row, rows, cols = places[3]
    a2 = maps_ref[row : row + rows, :][:, :cols]
    result = jnp.dot(a2, jnp.concatenate(blocks, axis=1), precision=EXACT,
                     preferred_element_type=jnp.float32)
    quarter_x, quarter_y, quarter_z = approx_ref.shape
    for s in range(slabs_two):
        bx, kx4 = divmod(s, quarter_x)
        block = result[:, s * lanes : (s + 1) * lanes]
        for by in range(2):
            for bz in range(2):
                piece = block[by * quarter_y : (by + 1) * quarter_y, bz * quarter_z : (bz + 1) * quarter_z]
                band = 4 * bx + 2 * by + bz
                if band:
                    two_out[band - 1, kx4] = piece
                else:
                    approx_ref[kx4] = piece


def y_pass(x_one, x_two, below, above, y_maps, places, nx, ny, nz):
    vmem = pl.BlockSpec(memory_space=pltpu.VMEM)
    lanes = x_one.shape[-1]
    return pl.pallas_call(
        functools.partial(y_pass_kernel, places=tuple(places)),
        out_shape=(
            jax.ShapeDtypeStruct((nx // 4, ny // 4, nz // 4), jnp.float32),
            jax.ShapeDtypeStruct((7, nx // 4, ny // 4, nz // 4), jnp.float32),
            jax.ShapeDtypeStruct((7, nx // 2, ny // 2, lanes), jnp.float32),
        ),
        in_specs=[vmem] * 5,
        out_specs=(vmem, vmem, vmem),
    )(x_one.reshape(-1, lanes), x_two.reshape(-1, lanes), below, above, y_maps)


def x_pass_kernel(own_ref, below_ref, above_ref, maps_ref, one_out, two_out, top_out, bottom_out, *,
                  taps, places, bands):
    ny = two_out.shape[0] // len(taps[1])
    slab = 2 * ny
    stride = bands * ny
    lo1, lo2 = 4, 12
    split = lo1 * slab

    def one_slab(i):
        if i < lo1:
            return below_ref[i * slab : (i + 1) * slab, :]
        if i < lo1 + ny:
            return own_ref[(i - lo1) * stride : (i - lo1) * stride + slab, :]
        j = i - lo1 - ny
        return above_ref[j * slab : (j + 1) * slab, :]

    def two_slab(i):
        if i < lo2:
            return below_ref[split + i * ny : split + (i + 1) * ny, :]
        if i < lo2 + ny:
            at = (i - lo2) * stride + slab
            return own_ref[at : at + ny, :]
        j = i - lo2 - ny
        return above_ref[split + j * ny : split + (j + 1) * ny, :]

    narrow = (top_out.shape[0] - two_out.shape[0]) // (len(taps[0]) * 2)
    row1 = places[0][0]
    for k, used in enumerate(taps[0]):
        acc = None
        for i in used:
            term = maps_ref[row1 + k, i] * one_slab(i)
            acc = term if acc is None else acc + term
        one_out[k * slab : (k + 1) * slab, :] = acc
        for b in range(2):
            at = (k * 2 + b) * narrow
            top_out[at : at + narrow, :] = acc[b * ny + ny - narrow : (b + 1) * ny, :]
            bottom_out[at : at + narrow, :] = acc[b * ny : b * ny + narrow, :]
    base = len(taps[0]) * 2 * narrow
    row2 = places[1][0]
    for k, used in enumerate(taps[1]):
        acc = None
        for i in used:
            term = maps_ref[row2 + k, i] * two_slab(i)
            acc = term if acc is None else acc + term
        two_out[k * ny : (k + 1) * ny, :] = acc
        top_out[base + k * ny : base + (k + 1) * ny, :] = acc
        bottom_out[base + k * ny : base + (k + 1) * ny, :] = acc


def used_taps(maps):
    present = np.any(np.stack([m != 0 for m in maps]), axis=0)
    return tuple(tuple(int(i) for i in np.nonzero(row)[0]) for row in present)


def x_pass(u, below, above, x_maps, places, nx, ny):
    lanes = u.shape[-1]
    taps = (used_taps(window_maps(nx, (4, 4), 0)), used_taps(window_maps(nx, (12, 12), 1)))
    narrow = 8
    vmem = pl.BlockSpec(memory_space=pltpu.VMEM)
    smem = pl.BlockSpec(memory_space=pltpu.SMEM)
    message = len(taps[0]) * 2 * narrow + len(taps[1]) * ny
    return pl.pallas_call(
        functools.partial(x_pass_kernel, taps=taps, places=tuple(places), bands=u.shape[1]),
        out_shape=(
            jax.ShapeDtypeStruct((len(taps[0]) * 2 * ny, lanes), jnp.float32),
            jax.ShapeDtypeStruct((len(taps[1]) * ny, lanes), jnp.float32),
            jax.ShapeDtypeStruct((message, lanes), jnp.float32),
            jax.ShapeDtypeStruct((message, lanes), jnp.float32),
        ),
        in_specs=[vmem, vmem, vmem, smem],
        out_specs=(vmem, vmem, vmem, vmem),
    )(u.reshape(-1, lanes), below, above, x_maps)


def per_device(velocity):
    nx, ny, nz = velocity.shape

    (z_low, z_high), (z2_low, z2_high) = level_maps(nz)
    z_maps = np.stack([z_low.T, z_high.T, np.concatenate([z2_low, z2_high]).T]).astype(np.float32)
    lanes = z_maps.shape[2]
    u = jnp.einsum("xyz,bzk->xbyk", velocity, jnp.asarray(z_maps), precision=EXACT)

    wide = 12
    below_raw, above_raw = exchange(velocity[:wide], velocity[nx - wide :], "slab")
    flat = lambda a: a.reshape(-1, lanes)
    near = jnp.stack([below_raw[wide - 4 :], above_raw[:4]])
    halo_one = jnp.einsum("hxyz,bzk->hxbyk", near, jnp.asarray(z_maps[0:2]), precision=EXACT)
    halo_two = jnp.einsum(
        "hxyz,zk->hxyk", jnp.stack([below_raw, above_raw]), jnp.asarray(z_maps[2]), precision=EXACT
    )
    below = jnp.concatenate([flat(halo_one[0]), flat(halo_two[0])])
    above = jnp.concatenate([flat(halo_one[1]), flat(halo_two[1])])
    assert nx == ny and wide == 12
    table, places = packed_maps(nx)
    table = jnp.asarray(table)
    x_maps = lax.dynamic_index_in_dim(table, case_of("slab"), keepdims=False)
    y_maps = lax.dynamic_index_in_dim(table, case_of("morton"), keepdims=False)
    x_one, x_two, top, bottom = x_pass(u, below, above, x_maps, places, nx, ny)

    below, above = exchange(bottom, top, "morton")
    return y_pass(x_one, x_two, below, above, y_maps, places, nx, ny, nz)


def solution(mesh):
    placed = (P("slab", "morton", None),)
    return jax.shard_map(
        per_device,
        mesh=mesh,
        in_specs=placed,
        out_specs=(
            P("slab", "morton", None),
            P(None, "slab", "morton", None),
            P(None, "slab", "morton", None),
        ),
        check_vma=False,
    )
```

```python
import functools

import numpy as np
import jax
import jax.numpy as jnp
from jax import lax
from jax.sharding import PartitionSpec as P
from jax.experimental import pallas as pl
from jax.experimental.pallas import tpu as pltpu

LIFT_ALPHA = -1.586134342059924
LIFT_BETA = -0.052980118572961
LIFT_GAMMA = 0.882911075530934
LIFT_DELTA = 0.443506852043971
LIFT_SCALE = 1.149604398860241

EXACT = lax.Precision.HIGHEST


def lift_rows(signal):
    extended = np.pad(signal, ((4, 4), (0, 0)), mode="reflect")
    even, odd = extended[0::2], extended[1::2]
    first_detail = odd[:-1] + LIFT_ALPHA * (even[:-1] + even[1:])
    first_smooth = even[1:-1] + LIFT_BETA * (first_detail[:-1] + first_detail[1:])
    second_detail = first_detail[1:-1] + LIFT_GAMMA * (first_smooth[:-1] + first_smooth[1:])
    second_smooth = first_smooth[1:-1] + LIFT_DELTA * (second_detail[:-1] + second_detail[1:])
    return second_smooth * LIFT_SCALE, second_detail[1:] / LIFT_SCALE


def level_maps(length):
    low, high = lift_rows(np.eye(length))
    low_two, high_two = lift_rows(low)
    return (low, high), (low_two, high_two)


def window_maps(block, halo, level, blocks=8):
    length = block * blocks
    bands = level_maps(length)[level]
    share = block // (2 * (level + 1))
    width = halo[0] + block + halo[1]
    maps = []
    for place in (0, blocks // 2, blocks - 1):
        rows = np.concatenate([band[place * share : (place + 1) * share] for band in bands])
        matrix = np.zeros((rows.shape[0], width))
        for i in range(width):
            cell = place * block - halo[0] + i
            if 0 <= cell < length:
                matrix[:, i] = rows[:, cell]
        maps.append(matrix.astype(np.float32))
    return maps


def packed_maps(block):
    parts = [
        window_maps(block, (4, 4), 0),
        window_maps(block, (12, 12), 1),
        window_maps(block, (8, 8), 0),
        window_maps(block, (block, block), 1),
    ]
    height = sum(p[0].shape[0] for p in parts)
    width = -(-max(p[0].shape[1] for p in parts) // 128) * 128
    table = np.zeros((3, height, width), np.float32)
    places, row = [], 0
    for p in parts:
        rows, cols = p[0].shape
        for case in range(3):
            table[case, row : row + rows, :cols] = p[case]
        places.append((row, rows, cols))
        row += rows
    return table, places


def case_of(axis):
    index = lax.axis_index(axis)
    last = lax.axis_size(axis) - 1
    return jnp.where(index == 0, 0, jnp.where(index == last, 2, 1))


def exchange(lower_half, upper_half, axis):
    devices = lax.axis_size(axis)
    up = [(i, i + 1) for i in range(devices - 1)]
    down = [(i + 1, i) for i in range(devices - 1)]
    from_below = lax.ppermute(upper_half, axis, up)
    from_above = lax.ppermute(lower_half, axis, down)
    return from_below, from_above


def y_pass_kernel(one_ref, two_ref, below_ref, above_ref, maps_ref, approx_ref, two_out, one_out, *, places):
    n_two, lanes = two_ref.shape
    n_one = one_ref.shape[0]
    ny = 2 * one_out.shape[2]
    slabs_one = n_one // ny
    slabs_two = n_two // ny
    narrow = (below_ref.shape[0] - n_two) // slabs_one
    blocks = []
    for s in range(slabs_one):
        blocks.append(
            jnp.concatenate(
                [
                    below_ref[s * narrow : (s + 1) * narrow, :],
                    one_ref[s * ny : (s + 1) * ny, :],
                    above_ref[s * narrow : (s + 1) * narrow, :],
                ]
            )
        )
    row, rows, cols = places[2]
    a1 = maps_ref[row : row + rows, :][:, :cols]
    result = jnp.dot(a1, jnp.concatenate(blocks, axis=1), precision=EXACT,
                     preferred_element_type=jnp.float32)
    half_x, half_y = one_out.shape[1], one_out.shape[2]
    for s in range(slabs_one):
        kx, bz = divmod(s, 2)
        bx, kx8 = divmod(kx, half_x)
        block = result[:, s * lanes : (s + 1) * lanes]
        for by in range(2):
            band = 4 * bx + 2 * by + bz
            if band:
                one_out[band - 1, kx8] = block[by * half_y : (by + 1) * half_y]
    base = n_one // ny * narrow
    blocks = []
    for s in range(slabs_two):
        blocks.append(
            jnp.concatenate(
                [
                    below_ref[base + s * ny : base + (s + 1) * ny, :],
                    two_ref[s * ny : (s + 1) * ny, :],
                    above_ref[base + s * ny : base + (s + 1) * ny, :],
                ]
            )
        )
    row, rows, cols = places[3]
    a2 = maps_ref[row : row + rows, :][:, :cols]
    result = jnp.dot(a2, jnp.concatenate(blocks, axis=1), precision=EXACT,
                     preferred_element_type=jnp.float32)
    quarter_x, quarter_y, quarter_z = approx_ref.shape
    for s in range(slabs_two):
        bx, kx4 = divmod(s, quarter_x)
        block = result[:, s * lanes : (s + 1) * lanes]
        for by in range(2):
            for bz in range(2):
                piece = block[by * quarter_y : (by + 1) * quarter_y, bz * quarter_z : (bz + 1) * quarter_z]
                band = 4 * bx + 2 * by + bz
                if band:
                    two_out[band - 1, kx4] = piece
                else:
                    approx_ref[kx4] = piece


def y_pass(x_one, x_two, below, above, y_maps, places, nx, ny, nz):
    vmem = pl.BlockSpec(memory_space=pltpu.VMEM)
    lanes = x_one.shape[-1]
    return pl.pallas_call(
        functools.partial(y_pass_kernel, places=tuple(places)),
        out_shape=(
            jax.ShapeDtypeStruct((nx // 4, ny // 4, nz // 4), jnp.float32),
            jax.ShapeDtypeStruct((7, nx // 4, ny // 4, nz // 4), jnp.float32),
            jax.ShapeDtypeStruct((7, nx // 2, ny // 2, lanes), jnp.float32),
        ),
        in_specs=[vmem] * 5,
        out_specs=(vmem, vmem, vmem),
    )(x_one.reshape(-1, lanes), x_two.reshape(-1, lanes), below, above, y_maps)


def x_pass_kernel(own_ref, near_ref, far_ref, maps_ref, one_out, two_out, top_out, bottom_out, *,
                  taps, places, bands):
    ny = two_out.shape[0] // len(taps[1])
    slab = 2 * ny
    stride = bands * ny
    lo1, lo2 = 4, 12
    side_one, side_two = lo1 * slab, lo2 * ny

    def one_slab(i):
        if i < lo1:
            return near_ref[i * slab : (i + 1) * slab, :]
        if i < lo1 + ny:
            return own_ref[(i - lo1) * stride : (i - lo1) * stride + slab, :]
        j = i - lo1 - ny
        return near_ref[side_one + j * slab : side_one + (j + 1) * slab, :]

    def two_slab(i):
        if i < lo2:
            return far_ref[i * ny : (i + 1) * ny, :]
        if i < lo2 + ny:
            at = (i - lo2) * stride + slab
            return own_ref[at : at + ny, :]
        j = i - lo2 - ny
        return far_ref[side_two + j * ny : side_two + (j + 1) * ny, :]

    narrow = (top_out.shape[0] - two_out.shape[0]) // (len(taps[0]) * 2)
    row1 = places[0][0]
    for k, used in enumerate(taps[0]):
        acc = None
        for i in used:
            term = maps_ref[row1 + k, i] * one_slab(i)
            acc = term if acc is None else acc + term
        one_out[k * slab : (k + 1) * slab, :] = acc
        for b in range(2):
            at = (k * 2 + b) * narrow
            top_out[at : at + narrow, :] = acc[b * ny + ny - narrow : (b + 1) * ny, :]
            bottom_out[at : at + narrow, :] = acc[b * ny : b * ny + narrow, :]
    base = len(taps[0]) * 2 * narrow
    row2 = places[1][0]
    for k, used in enumerate(taps[1]):
        acc = None
        for i in used:
            term = maps_ref[row2 + k, i] * two_slab(i)
            acc = term if acc is None else acc + term
        two_out[k * ny : (k + 1) * ny, :] = acc
        top_out[base + k * ny : base + (k + 1) * ny, :] = acc
        bottom_out[base + k * ny : base + (k + 1) * ny, :] = acc


def used_taps(maps):
    present = np.any(np.stack([m != 0 for m in maps]), axis=0)
    return tuple(tuple(int(i) for i in np.nonzero(row)[0]) for row in present)


def x_pass(u, near, far, x_maps, places, nx, ny):
    lanes = u.shape[-1]
    taps = (used_taps(window_maps(nx, (4, 4), 0)), used_taps(window_maps(nx, (12, 12), 1)))
    narrow = 8
    vmem = pl.BlockSpec(memory_space=pltpu.VMEM)
    smem = pl.BlockSpec(memory_space=pltpu.SMEM)
    message = len(taps[0]) * 2 * narrow + len(taps[1]) * ny
    return pl.pallas_call(
        functools.partial(x_pass_kernel, taps=taps, places=tuple(places), bands=u.shape[1]),
        out_shape=(
            jax.ShapeDtypeStruct((len(taps[0]) * 2 * ny, lanes), jnp.float32),
            jax.ShapeDtypeStruct((len(taps[1]) * ny, lanes), jnp.float32),
            jax.ShapeDtypeStruct((message, lanes), jnp.float32),
            jax.ShapeDtypeStruct((message, lanes), jnp.float32),
        ),
        in_specs=[vmem, vmem, vmem, smem],
        out_specs=(vmem, vmem, vmem, vmem),
    )(u.reshape(-1, lanes), near.reshape(-1, lanes), far.reshape(-1, lanes), x_maps)


def per_device(velocity):
    nx, ny, nz = velocity.shape

    (z_low, z_high), (z2_low, z2_high) = level_maps(nz)
    z_maps = np.stack([z_low.T, z_high.T, np.concatenate([z2_low, z2_high]).T]).astype(np.float32)
    lanes = z_maps.shape[2]
    u = jnp.einsum("xyz,bzk->xbyk", velocity, jnp.asarray(z_maps), precision=EXACT)

    wide = 12
    below_raw, above_raw = exchange(velocity[:wide], velocity[nx - wide :], "slab")
    flat = lambda a: a.reshape(-1, lanes)
    near = jnp.stack([below_raw[wide - 4 :], above_raw[:4]])
    halo_one = jnp.einsum("hxyz,bzk->hxbyk", near, jnp.asarray(z_maps[0:2]), precision=EXACT)
    halo_two = jnp.einsum(
        "hxyz,zk->hxyk", jnp.stack([below_raw, above_raw]), jnp.asarray(z_maps[2]), precision=EXACT
    )
    assert nx == ny and wide == 12
    table, places = packed_maps(nx)
    table = jnp.asarray(table)
    x_maps = lax.dynamic_index_in_dim(table, case_of("slab"), keepdims=False)
    y_maps = lax.dynamic_index_in_dim(table, case_of("morton"), keepdims=False)
    x_one, x_two, top, bottom = x_pass(u, halo_one, halo_two, x_maps, places, nx, ny)

    below, above = exchange(bottom, top, "morton")
    return y_pass(x_one, x_two, below, above, y_maps, places, nx, ny, nz)


def solution(mesh):
    placed = (P("slab", "morton", None),)
    return jax.shard_map(
        per_device,
        mesh=mesh,
        in_specs=placed,
        out_specs=(
            P("slab", "morton", None),
            P(None, "slab", "morton", None),
            P(None, "slab", "morton", None),
        ),
        check_vma=False,
    )
```

```python
import functools

import numpy as np
import jax
import jax.numpy as jnp
from jax import lax
from jax.sharding import PartitionSpec as P
from jax.experimental import pallas as pl
from jax.experimental.pallas import tpu as pltpu

LIFT_ALPHA = -1.586134342059924
LIFT_BETA = -0.052980118572961
LIFT_GAMMA = 0.882911075530934
LIFT_DELTA = 0.443506852043971
LIFT_SCALE = 1.149604398860241

EXACT = lax.Precision.HIGHEST


def lift_rows(signal):
    extended = np.pad(signal, ((4, 4), (0, 0)), mode="reflect")
    even, odd = extended[0::2], extended[1::2]
    first_detail = odd[:-1] + LIFT_ALPHA * (even[:-1] + even[1:])
    first_smooth = even[1:-1] + LIFT_BETA * (first_detail[:-1] + first_detail[1:])
    second_detail = first_detail[1:-1] + LIFT_GAMMA * (first_smooth[:-1] + first_smooth[1:])
    second_smooth = first_smooth[1:-1] + LIFT_DELTA * (second_detail[:-1] + second_detail[1:])
    return second_smooth * LIFT_SCALE, second_detail[1:] / LIFT_SCALE


def level_maps(length):
    low, high = lift_rows(np.eye(length))
    low_two, high_two = lift_rows(low)
    return (low, high), (low_two, high_two)


def window_maps(block, halo, level, blocks=8):
    length = block * blocks
    bands = level_maps(length)[level]
    share = block // (2 * (level + 1))
    width = halo[0] + block + halo[1]
    maps = []
    for place in (0, blocks // 2, blocks - 1):
        rows = np.concatenate([band[place * share : (place + 1) * share] for band in bands])
        matrix = np.zeros((rows.shape[0], width))
        for i in range(width):
            cell = place * block - halo[0] + i
            if 0 <= cell < length:
                matrix[:, i] = rows[:, cell]
        maps.append(matrix.astype(np.float32))
    return maps


def packed_maps(block):
    parts = [
        window_maps(block, (4, 4), 0),
        window_maps(block, (12, 12), 1),
        window_maps(block, (8, 8), 0),
        window_maps(block, (block, block), 1),
    ]
    height = sum(p[0].shape[0] for p in parts)
    width = -(-max(p[0].shape[1] for p in parts) // 128) * 128
    table = np.zeros((3, height, width), np.float32)
    places, row = [], 0
    for p in parts:
        rows, cols = p[0].shape
        for case in range(3):
            table[case, row : row + rows, :cols] = p[case]
        places.append((row, rows, cols))
        row += rows
    return table, places


def case_of(axis):
    index = lax.axis_index(axis)
    last = lax.axis_size(axis) - 1
    return jnp.where(index == 0, 0, jnp.where(index == last, 2, 1))


def exchange(lower_half, upper_half, axis):
    devices = lax.axis_size(axis)
    up = [(i, i + 1) for i in range(devices - 1)]
    down = [(i + 1, i) for i in range(devices - 1)]
    from_below = lax.ppermute(upper_half, axis, up)
    from_above = lax.ppermute(lower_half, axis, down)
    return from_below, from_above


def y_pass_kernel(one_ref, two_ref, below_ref, above_ref, maps_ref, approx_ref, two_out, one_out, *, places):
    n_two, lanes = two_ref.shape
    n_one = one_ref.shape[0]
    ny = 2 * one_out.shape[2]
    slabs_one = n_one // ny
    slabs_two = n_two // ny
    narrow = (below_ref.shape[0] - n_two) // slabs_one
    blocks = []
    for s in range(slabs_one):
        blocks.append(
            jnp.concatenate(
                [
                    below_ref[s * narrow : (s + 1) * narrow, :],
                    one_ref[s * ny : (s + 1) * ny, :],
                    above_ref[s * narrow : (s + 1) * narrow, :],
                ]
            )
        )
    row, rows, cols = places[2]
    a1 = maps_ref[row : row + rows, :][:, :cols]
    result = jnp.dot(a1, jnp.concatenate(blocks, axis=1), precision=EXACT,
                     preferred_element_type=jnp.float32)
    half_x, half_y = one_out.shape[1], one_out.shape[2]
    for s in range(slabs_one):
        kx, bz = divmod(s, 2)
        bx, kx8 = divmod(kx, half_x)
        block = result[:, s * lanes : (s + 1) * lanes]
        for by in range(2):
            band = 4 * bx + 2 * by + bz
            if band:
                one_out[band - 1, kx8] = block[by * half_y : (by + 1) * half_y]
    base = n_one // ny * narrow
    blocks = []
    for s in range(slabs_two):
        blocks.append(
            jnp.concatenate(
                [
                    below_ref[base + s * ny : base + (s + 1) * ny, :],
                    two_ref[s * ny : (s + 1) * ny, :],
                    above_ref[base + s * ny : base + (s + 1) * ny, :],
                ]
            )
        )
    row, rows, cols = places[3]
    a2 = maps_ref[row : row + rows, :][:, :cols]
    result = jnp.dot(a2, jnp.concatenate(blocks, axis=1), precision=EXACT,
                     preferred_element_type=jnp.float32)
    quarter_x, quarter_y, quarter_z = approx_ref.shape
    for s in range(slabs_two):
        bx, kx4 = divmod(s, quarter_x)
        block = result[:, s * lanes : (s + 1) * lanes]
        for by in range(2):
            for bz in range(2):
                piece = block[by * quarter_y : (by + 1) * quarter_y, bz * quarter_z : (bz + 1) * quarter_z]
                band = 4 * bx + 2 * by + bz
                if band:
                    two_out[band - 1, kx4] = piece
                else:
                    approx_ref[kx4] = piece


def y_pass(x_one, x_two, below, above, y_maps, places, nx, ny, nz):
    vmem = pl.BlockSpec(memory_space=pltpu.VMEM)
    lanes = x_one.shape[-1]
    return pl.pallas_call(
        functools.partial(y_pass_kernel, places=tuple(places)),
        out_shape=(
            jax.ShapeDtypeStruct((nx // 4, ny // 4, nz // 4), jnp.float32),
            jax.ShapeDtypeStruct((7, nx // 4, ny // 4, nz // 4), jnp.float32),
            jax.ShapeDtypeStruct((7, nx // 2, ny // 2, lanes), jnp.float32),
        ),
        in_specs=[vmem] * 5,
        out_specs=(vmem, vmem, vmem),
    )(x_one.reshape(-1, lanes), x_two.reshape(-1, lanes), below, above, y_maps)


def z_pass_kernel(v_ref, z_ref, u_out, top_out, bottom_out, *, rows_one, rows_two):
    lanes = u_out.shape[1]
    bands = z_ref.shape[1] // lanes
    ny = top_out.shape[0] // (rows_one * 2 + rows_two)
    nx = v_ref.shape[0] // ny
    result = jnp.dot(v_ref[...], z_ref[...], precision=EXACT, preferred_element_type=jnp.float32)
    split = rows_one * 2 * ny
    for x in range(nx):
        for b in range(bands):
            block = result[x * ny : (x + 1) * ny, b * lanes : (b + 1) * lanes]
            u_out[(x * bands + b) * ny : (x * bands + b + 1) * ny, :] = block
            if b < 2:
                if x >= nx - rows_one:
                    at = ((x - nx + rows_one) * 2 + b) * ny
                    top_out[at : at + ny, :] = block
                if x < rows_one:
                    at = (x * 2 + b) * ny
                    bottom_out[at : at + ny, :] = block
            else:
                if x >= nx - rows_two:
                    at = split + (x - nx + rows_two) * ny
                    top_out[at : at + ny, :] = block
                if x < rows_two:
                    at = split + x * ny
                    bottom_out[at : at + ny, :] = block


def z_pass(velocity, z_maps, rows_one, rows_two):
    nx, ny, nz = velocity.shape
    lanes = z_maps.shape[2]
    bands = z_maps.shape[0]
    matrix = np.concatenate(list(z_maps), axis=1)
    vmem = pl.BlockSpec(memory_space=pltpu.VMEM)
    message = (rows_one * 2 + rows_two) * ny
    return pl.pallas_call(
        functools.partial(z_pass_kernel, rows_one=rows_one, rows_two=rows_two),
        out_shape=(
            jax.ShapeDtypeStruct((nx * bands * ny, lanes), jnp.float32),
            jax.ShapeDtypeStruct((message, lanes), jnp.float32),
            jax.ShapeDtypeStruct((message, lanes), jnp.float32),
        ),
        in_specs=[vmem, vmem],
        out_specs=(vmem, vmem, vmem),
    )(velocity.reshape(nx * ny, nz), jnp.asarray(matrix))


def x_pass_kernel(own_ref, below_ref, above_ref, maps_ref, one_out, two_out, top_out, bottom_out, *,
                  taps, places, bands):
    ny = two_out.shape[0] // len(taps[1])
    slab = 2 * ny
    stride = bands * ny
    lo1, lo2 = 4, 12
    split = lo1 * slab

    def one_slab(i):
        if i < lo1:
            return below_ref[i * slab : (i + 1) * slab, :]
        if i < lo1 + ny:
            return own_ref[(i - lo1) * stride : (i - lo1) * stride + slab, :]
        j = i - lo1 - ny
        return above_ref[j * slab : (j + 1) * slab, :]

    def two_slab(i):
        if i < lo2:
            return below_ref[split + i * ny : split + (i + 1) * ny, :]
        if i < lo2 + ny:
            at = (i - lo2) * stride + slab
            return own_ref[at : at + ny, :]
        j = i - lo2 - ny
        return above_ref[split + j * ny : split + (j + 1) * ny, :]

    narrow = (top_out.shape[0] - two_out.shape[0]) // (len(taps[0]) * 2)
    row1 = places[0][0]
    for k, used in enumerate(taps[0]):
        acc = None
        for i in used:
            term = maps_ref[row1 + k, i] * one_slab(i)
            acc = term if acc is None else acc + term
        one_out[k * slab : (k + 1) * slab, :] = acc
        for b in range(2):
            at = (k * 2 + b) * narrow
            top_out[at : at + narrow, :] = acc[b * ny + ny - narrow : (b + 1) * ny, :]
            bottom_out[at : at + narrow, :] = acc[b * ny : b * ny + narrow, :]
    base = len(taps[0]) * 2 * narrow
    row2 = places[1][0]
    for k, used in enumerate(taps[1]):
        acc = None
        for i in used:
            term = maps_ref[row2 + k, i] * two_slab(i)
            acc = term if acc is None else acc + term
        two_out[k * ny : (k + 1) * ny, :] = acc
        top_out[base + k * ny : base + (k + 1) * ny, :] = acc
        bottom_out[base + k * ny : base + (k + 1) * ny, :] = acc


def used_taps(maps):
    present = np.any(np.stack([m != 0 for m in maps]), axis=0)
    return tuple(tuple(int(i) for i in np.nonzero(row)[0]) for row in present)


def x_pass(u, below, above, x_maps, places, nx, ny):
    lanes = u.shape[-1]
    taps = (used_taps(window_maps(nx, (4, 4), 0)), used_taps(window_maps(nx, (12, 12), 1)))
    narrow = 8
    vmem = pl.BlockSpec(memory_space=pltpu.VMEM)
    smem = pl.BlockSpec(memory_space=pltpu.SMEM)
    message = len(taps[0]) * 2 * narrow + len(taps[1]) * ny
    return pl.pallas_call(
        functools.partial(x_pass_kernel, taps=taps, places=tuple(places), bands=3),
        out_shape=(
            jax.ShapeDtypeStruct((len(taps[0]) * 2 * ny, lanes), jnp.float32),
            jax.ShapeDtypeStruct((len(taps[1]) * ny, lanes), jnp.float32),
            jax.ShapeDtypeStruct((message, lanes), jnp.float32),
            jax.ShapeDtypeStruct((message, lanes), jnp.float32),
        ),
        in_specs=[vmem, vmem, vmem, smem],
        out_specs=(vmem, vmem, vmem, vmem),
    )(u, below, above, x_maps)


def per_device(velocity):
    nx, ny, nz = velocity.shape

    (z_low, z_high), (z2_low, z2_high) = level_maps(nz)
    z_maps = np.stack([z_low.T, z_high.T, np.concatenate([z2_low, z2_high]).T]).astype(np.float32)
    lanes = z_maps.shape[2]
    wide = 12
    u, top, bottom = z_pass(velocity, z_maps, 4, wide)

    below, above = exchange(bottom, top, "slab")
    assert nx == ny and wide == 12
    table, places = packed_maps(nx)
    table = jnp.asarray(table)
    x_maps = lax.dynamic_index_in_dim(table, case_of("slab"), keepdims=False)
    y_maps = lax.dynamic_index_in_dim(table, case_of("morton"), keepdims=False)
    x_one, x_two, top, bottom = x_pass(u, below, above, x_maps, places, nx, ny)

    below, above = exchange(bottom, top, "morton")
    return y_pass(x_one, x_two, below, above, y_maps, places, nx, ny, nz)


def solution(mesh):
    placed = (P("slab", "morton", None),)
    return jax.shard_map(
        per_device,
        mesh=mesh,
        in_specs=placed,
        out_specs=(
            P("slab", "morton", None),
            P(None, "slab", "morton", None),
            P(None, "slab", "morton", None),
        ),
        check_vma=False,
    )
```

```python
import functools

import numpy as np
import jax
import jax.numpy as jnp
from jax import lax
from jax.sharding import PartitionSpec as P
from jax.experimental import pallas as pl
from jax.experimental.pallas import tpu as pltpu

LIFT_ALPHA = -1.586134342059924
LIFT_BETA = -0.052980118572961
LIFT_GAMMA = 0.882911075530934
LIFT_DELTA = 0.443506852043971
LIFT_SCALE = 1.149604398860241

EXACT = lax.Precision.HIGHEST


def lift_rows(signal):
    extended = np.pad(signal, ((4, 4), (0, 0)), mode="reflect")
    even, odd = extended[0::2], extended[1::2]
    first_detail = odd[:-1] + LIFT_ALPHA * (even[:-1] + even[1:])
    first_smooth = even[1:-1] + LIFT_BETA * (first_detail[:-1] + first_detail[1:])
    second_detail = first_detail[1:-1] + LIFT_GAMMA * (first_smooth[:-1] + first_smooth[1:])
    second_smooth = first_smooth[1:-1] + LIFT_DELTA * (second_detail[:-1] + second_detail[1:])
    return second_smooth * LIFT_SCALE, second_detail[1:] / LIFT_SCALE


def level_maps(length):
    low, high = lift_rows(np.eye(length))
    low_two, high_two = lift_rows(low)
    return (low, high), (low_two, high_two)


def window_maps(block, halo, level, blocks=8):
    length = block * blocks
    bands = level_maps(length)[level]
    share = block // (2 * (level + 1))
    width = halo[0] + block + halo[1]
    maps = []
    for place in (0, blocks // 2, blocks - 1):
        rows = np.concatenate([band[place * share : (place + 1) * share] for band in bands])
        matrix = np.zeros((rows.shape[0], width))
        for i in range(width):
            cell = place * block - halo[0] + i
            if 0 <= cell < length:
                matrix[:, i] = rows[:, cell]
        maps.append(matrix.astype(np.float32))
    return maps


def packed_maps(block):
    parts = [
        window_maps(block, (4, 4), 0),
        window_maps(block, (12, 12), 1),
        window_maps(block, (8, 8), 0),
        window_maps(block, (block, block), 1),
    ]
    height = sum(p[0].shape[0] for p in parts)
    width = -(-max(p[0].shape[1] for p in parts) // 128) * 128
    table = np.zeros((3, height, width), np.float32)
    places, row = [], 0
    for p in parts:
        rows, cols = p[0].shape
        for case in range(3):
            table[case, row : row + rows, :cols] = p[case]
        places.append((row, rows, cols))
        row += rows
    return table, places


def case_of(axis):
    index = lax.axis_index(axis)
    last = lax.axis_size(axis) - 1
    return jnp.where(index == 0, 0, jnp.where(index == last, 2, 1))


def exchange(lower_half, upper_half, axis):
    devices = lax.axis_size(axis)
    up = [(i, i + 1) for i in range(devices - 1)]
    down = [(i + 1, i) for i in range(devices - 1)]
    from_below = lax.ppermute(upper_half, axis, up)
    from_above = lax.ppermute(lower_half, axis, down)
    return from_below, from_above


def y_pass_kernel(one_ref, two_ref, below_ref, above_ref, maps_ref, approx_ref, two_out, one_out, *, places):
    n_two, lanes = two_ref.shape
    n_one = one_ref.shape[0]
    ny = 2 * one_out.shape[2]
    slabs_one = n_one // ny
    slabs_two = n_two // ny
    narrow, wide = 4, 12
    blocks = []
    for s in range(slabs_one):
        blocks.append(
            jnp.concatenate(
                [
                    below_ref[s * narrow : (s + 1) * narrow, :],
                    one_ref[s * ny : (s + 1) * ny, :],
                    above_ref[s * narrow : (s + 1) * narrow, :],
                ]
            )
        )
    row, rows, cols = places[0]
    a1 = maps_ref[row : row + rows, :][:, :cols]
    result = jnp.dot(a1, jnp.concatenate(blocks, axis=1), precision=EXACT,
                     preferred_element_type=jnp.float32)
    half_x, half_y = one_out.shape[1], one_out.shape[2]
    for s in range(slabs_one):
        kx, bz = divmod(s, 2)
        bx, kx8 = divmod(kx, half_x)
        block = result[:, s * lanes : (s + 1) * lanes]
        for by in range(2):
            band = 4 * bx + 2 * by + bz
            if band:
                one_out[band - 1, kx8] = block[by * half_y : (by + 1) * half_y]
    base = n_one // ny * narrow
    blocks = []
    for s in range(slabs_two):
        blocks.append(
            jnp.concatenate(
                [
                    below_ref[base + s * wide : base + (s + 1) * wide, :],
                    two_ref[s * ny : (s + 1) * ny, :],
                    above_ref[base + s * wide : base + (s + 1) * wide, :],
                ]
            )
        )
    row, rows, cols = places[1]
    a2 = maps_ref[row : row + rows, :][:, :cols]
    result = jnp.dot(a2, jnp.concatenate(blocks, axis=1), precision=EXACT,
                     preferred_element_type=jnp.float32)
    quarter_x, quarter_y, quarter_z = approx_ref.shape
    for s in range(slabs_two):
        bx, kx4 = divmod(s, quarter_x)
        block = result[:, s * lanes : (s + 1) * lanes]
        for by in range(2):
            for bz in range(2):
                piece = block[by * quarter_y : (by + 1) * quarter_y, bz * quarter_z : (bz + 1) * quarter_z]
                band = 4 * bx + 2 * by + bz
                if band:
                    two_out[band - 1, kx4] = piece
                else:
                    approx_ref[kx4] = piece


def y_pass(x_one, x_two, below, above, y_maps, places, nx, ny, nz):
    vmem = pl.BlockSpec(memory_space=pltpu.VMEM)
    lanes = x_one.shape[-1]
    return pl.pallas_call(
        functools.partial(y_pass_kernel, places=tuple(places)),
        out_shape=(
            jax.ShapeDtypeStruct((nx // 4, ny // 4, nz // 4), jnp.float32),
            jax.ShapeDtypeStruct((7, nx // 4, ny // 4, nz // 4), jnp.float32),
            jax.ShapeDtypeStruct((7, nx // 2, ny // 2, lanes), jnp.float32),
        ),
        in_specs=[vmem] * 5,
        out_specs=(vmem, vmem, vmem),
    )(x_one.reshape(-1, lanes), x_two.reshape(-1, lanes), below, above, y_maps)


def x_pass_kernel(own_ref, below_ref, above_ref, maps_ref, one_out, two_out, top_out, bottom_out, *,
                  taps, places, bands):
    ny = two_out.shape[0] // len(taps[1])
    slab = 2 * ny
    stride = bands * ny
    lo1, lo2 = 4, 12
    split = lo1 * slab

    def one_slab(i):
        if i < lo1:
            return below_ref[i * slab : (i + 1) * slab, :]
        if i < lo1 + ny:
            return own_ref[(i - lo1) * stride : (i - lo1) * stride + slab, :]
        j = i - lo1 - ny
        return above_ref[j * slab : (j + 1) * slab, :]

    def two_slab(i):
        if i < lo2:
            return below_ref[split + i * ny : split + (i + 1) * ny, :]
        if i < lo2 + ny:
            at = (i - lo2) * stride + slab
            return own_ref[at : at + ny, :]
        j = i - lo2 - ny
        return above_ref[split + j * ny : split + (j + 1) * ny, :]

    narrow, wide = lo1, lo2
    row1 = places[0][0]
    for k, used in enumerate(taps[0]):
        acc = None
        for i in used:
            term = maps_ref[row1 + k, i] * one_slab(i)
            acc = term if acc is None else acc + term
        one_out[k * slab : (k + 1) * slab, :] = acc
        for b in range(2):
            at = (k * 2 + b) * narrow
            top_out[at : at + narrow, :] = acc[b * ny + ny - narrow : (b + 1) * ny, :]
            bottom_out[at : at + narrow, :] = acc[b * ny : b * ny + narrow, :]
    base = len(taps[0]) * 2 * narrow
    row2 = places[1][0]
    for k, used in enumerate(taps[1]):
        acc = None
        for i in used:
            term = maps_ref[row2 + k, i] * two_slab(i)
            acc = term if acc is None else acc + term
        two_out[k * ny : (k + 1) * ny, :] = acc
        top_out[base + k * wide : base + (k + 1) * wide, :] = acc[ny - wide :, :]
        bottom_out[base + k * wide : base + (k + 1) * wide, :] = acc[:wide, :]


def used_taps(maps):
    present = np.any(np.stack([m != 0 for m in maps]), axis=0)
    return tuple(tuple(int(i) for i in np.nonzero(row)[0]) for row in present)


def x_pass(u, below, above, x_maps, places, nx, ny):
    lanes = u.shape[-1]
    taps = (used_taps(window_maps(nx, (4, 4), 0)), used_taps(window_maps(nx, (12, 12), 1)))
    narrow, wide = 4, 12
    vmem = pl.BlockSpec(memory_space=pltpu.VMEM)
    smem = pl.BlockSpec(memory_space=pltpu.SMEM)
    message = len(taps[0]) * 2 * narrow + len(taps[1]) * wide
    return pl.pallas_call(
        functools.partial(x_pass_kernel, taps=taps, places=tuple(places), bands=u.shape[1]),
        out_shape=(
            jax.ShapeDtypeStruct((len(taps[0]) * 2 * ny, lanes), jnp.float32),
            jax.ShapeDtypeStruct((len(taps[1]) * ny, lanes), jnp.float32),
            jax.ShapeDtypeStruct((message, lanes), jnp.float32),
            jax.ShapeDtypeStruct((message, lanes), jnp.float32),
        ),
        in_specs=[vmem, vmem, vmem, smem],
        out_specs=(vmem, vmem, vmem, vmem),
    )(u.reshape(-1, lanes), below, above, x_maps)


def per_device(velocity):
    nx, ny, nz = velocity.shape

    (z_low, z_high), (z2_low, z2_high) = level_maps(nz)
    z_maps = np.stack([z_low.T, z_high.T, np.concatenate([z2_low, z2_high]).T]).astype(np.float32)
    lanes = z_maps.shape[2]
    u = jnp.einsum("xyz,bzk->xbyk", velocity, jnp.asarray(z_maps), precision=EXACT)

    wide = 12
    one_rows = u[:, 0:2]
    two_rows = u[:, 2]
    flat = lambda a: a.reshape(-1, lanes)
    top = jnp.concatenate([flat(one_rows[nx - 4 :]), flat(two_rows[nx - wide :])])
    bottom = jnp.concatenate([flat(one_rows[:4]), flat(two_rows[:wide])])
    below, above = exchange(bottom, top, "slab")
    assert nx == ny and wide == 12
    table, places = packed_maps(nx)
    table = jnp.asarray(table)
    x_maps = lax.dynamic_index_in_dim(table, case_of("slab"), keepdims=False)
    y_maps = lax.dynamic_index_in_dim(table, case_of("morton"), keepdims=False)
    x_one, x_two, top, bottom = x_pass(u, below, above, x_maps, places, nx, ny)

    below, above = exchange(bottom, top, "morton")
    return y_pass(x_one, x_two, below, above, y_maps, places, nx, ny, nz)


def solution(mesh):
    placed = (P("slab", "morton", None),)
    return jax.shard_map(
        per_device,
        mesh=mesh,
        in_specs=placed,
        out_specs=(
            P("slab", "morton", None),
            P(None, "slab", "morton", None),
            P(None, "slab", "morton", None),
        ),
        check_vma=False,
    )
```

```python
import functools

import numpy as np
import jax
import jax.numpy as jnp
from jax import lax
from jax.sharding import PartitionSpec as P
from jax.experimental import pallas as pl
from jax.experimental.pallas import tpu as pltpu

LIFT_ALPHA = -1.586134342059924
LIFT_BETA = -0.052980118572961
LIFT_GAMMA = 0.882911075530934
LIFT_DELTA = 0.443506852043971
LIFT_SCALE = 1.149604398860241

EXACT = lax.Precision.HIGHEST


def lift_rows(signal):
    extended = np.pad(signal, ((4, 4), (0, 0)), mode="reflect")
    even, odd = extended[0::2], extended[1::2]
    first_detail = odd[:-1] + LIFT_ALPHA * (even[:-1] + even[1:])
    first_smooth = even[1:-1] + LIFT_BETA * (first_detail[:-1] + first_detail[1:])
    second_detail = first_detail[1:-1] + LIFT_GAMMA * (first_smooth[:-1] + first_smooth[1:])
    second_smooth = first_smooth[1:-1] + LIFT_DELTA * (second_detail[:-1] + second_detail[1:])
    return second_smooth * LIFT_SCALE, second_detail[1:] / LIFT_SCALE


def level_maps(length):
    low, high = lift_rows(np.eye(length))
    low_two, high_two = lift_rows(low)
    return (low, high), (low_two, high_two)


def window_maps(block, halo, level, blocks=8):
    length = block * blocks
    bands = level_maps(length)[level]
    share = block // (2 * (level + 1))
    width = halo[0] + block + halo[1]
    maps = []
    for place in (0, blocks // 2, blocks - 1):
        rows = np.concatenate([band[place * share : (place + 1) * share] for band in bands])
        matrix = np.zeros((rows.shape[0], width))
        for i in range(width):
            cell = place * block - halo[0] + i
            if 0 <= cell < length:
                matrix[:, i] = rows[:, cell]
        maps.append(matrix.astype(np.float32))
    return maps


def packed_maps(block):
    parts = [
        window_maps(block, (4, 4), 0),
        window_maps(block, (12, 12), 1),
        window_maps(block, (8, 8), 0),
        window_maps(block, (block, block), 1),
    ]
    height = sum(p[0].shape[0] for p in parts)
    width = -(-max(p[0].shape[1] for p in parts) // 128) * 128
    table = np.zeros((3, height, width), np.float32)
    places, row = [], 0
    for p in parts:
        rows, cols = p[0].shape
        for case in range(3):
            table[case, row : row + rows, :cols] = p[case]
        places.append((row, rows, cols))
        row += rows
    return table, places


def case_of(axis):
    index = lax.axis_index(axis)
    last = lax.axis_size(axis) - 1
    return jnp.where(index == 0, 0, jnp.where(index == last, 2, 1))


def exchange(lower_half, upper_half, axis):
    devices = lax.axis_size(axis)
    up = [(i, i + 1) for i in range(devices - 1)]
    down = [(i + 1, i) for i in range(devices - 1)]
    from_below = lax.ppermute(upper_half, axis, up)
    from_above = lax.ppermute(lower_half, axis, down)
    return from_below, from_above


def y_pass_kernel(one_ref, two_ref, below_ref, above_ref, maps_ref, approx_ref, two_out, one_out, *, places):
    n_two, lanes = two_ref.shape
    n_one = one_ref.shape[0]
    ny = 2 * one_out.shape[2]
    slabs_one = n_one // ny
    slabs_two = n_two // ny
    narrow, wide = 4, 12
    blocks = []
    for s in range(slabs_one):
        blocks.append(
            jnp.concatenate(
                [
                    below_ref[s * narrow : (s + 1) * narrow, :],
                    one_ref[s * ny : (s + 1) * ny, :],
                    above_ref[s * narrow : (s + 1) * narrow, :],
                ]
            )
        )
    row, rows, cols = places[0]
    a1 = maps_ref[row : row + rows, :][:, :cols]
    result = jnp.dot(a1, jnp.concatenate(blocks, axis=1), precision=EXACT,
                     preferred_element_type=jnp.float32)
    half_x, half_y = one_out.shape[1], one_out.shape[2]
    for s in range(slabs_one):
        kx, bz = divmod(s, 2)
        bx, kx8 = divmod(kx, half_x)
        block = result[:, s * lanes : (s + 1) * lanes]
        for by in range(2):
            band = 4 * bx + 2 * by + bz
            if band:
                one_out[band - 1, kx8] = block[by * half_y : (by + 1) * half_y]
    base = n_one // ny * narrow
    blocks = []
    for s in range(slabs_two):
        blocks.append(
            jnp.concatenate(
                [
                    below_ref[base + s * wide : base + (s + 1) * wide, :],
                    two_ref[s * ny : (s + 1) * ny, :],
                    above_ref[base + s * wide : base + (s + 1) * wide, :],
                ]
            )
        )
    row, rows, cols = places[1]
    a2 = maps_ref[row : row + rows, :][:, :cols]
    result = jnp.dot(a2, jnp.concatenate(blocks, axis=1), precision=EXACT,
                     preferred_element_type=jnp.float32)
    quarter_x, quarter_y, quarter_z = approx_ref.shape
    for s in range(slabs_two):
        bx, kx4 = divmod(s, quarter_x)
        block = result[:, s * lanes : (s + 1) * lanes]
        for by in range(2):
            for bz in range(2):
                piece = block[by * quarter_y : (by + 1) * quarter_y, bz * quarter_z : (bz + 1) * quarter_z]
                band = 4 * bx + 2 * by + bz
                if band:
                    two_out[band - 1, kx4] = piece
                else:
                    approx_ref[kx4] = piece


def y_pass(x_one, x_two, below, above, y_maps, places, nx, ny, nz):
    vmem = pl.BlockSpec(memory_space=pltpu.VMEM)
    lanes = x_one.shape[-1]
    return pl.pallas_call(
        functools.partial(y_pass_kernel, places=tuple(places)),
        out_shape=(
            jax.ShapeDtypeStruct((nx // 4, ny // 4, nz // 4), jnp.float32),
            jax.ShapeDtypeStruct((7, nx // 4, ny // 4, nz // 4), jnp.float32),
            jax.ShapeDtypeStruct((7, nx // 2, ny // 2, lanes), jnp.float32),
        ),
        in_specs=[vmem] * 5,
        out_specs=(vmem, vmem, vmem),
    )(x_one.reshape(-1, lanes), x_two.reshape(-1, lanes), below, above, y_maps)


def x_pass_kernel(edge_ref, middle_ref, coarse_ref, below_ref, above_ref, maps_ref, one_out, two_out,
                  top_out, bottom_out, *, taps, places):
    ny = two_out.shape[0] // len(taps[1])
    slab = 2 * ny
    nx = coarse_ref.shape[0] // ny
    lo1, lo2 = 4, 12
    split = lo1 * slab

    def one_slab(i):
        if i < lo1:
            return below_ref[i * slab : (i + 1) * slab, :]
        if i < lo1 + ny:
            x = i - lo1
            if x < lo1:
                return edge_ref[x * slab : (x + 1) * slab, :]
            if x >= nx - lo1:
                x = x - nx + 2 * lo1
                return edge_ref[x * slab : (x + 1) * slab, :]
            x = x - lo1
            return middle_ref[x * slab : (x + 1) * slab, :]
        j = i - lo1 - ny
        return above_ref[j * slab : (j + 1) * slab, :]

    def two_slab(i):
        if i < lo2:
            return below_ref[split + i * ny : split + (i + 1) * ny, :]
        if i < lo2 + ny:
            at = (i - lo2) * ny
            return coarse_ref[at : at + ny, :]
        j = i - lo2 - ny
        return above_ref[split + j * ny : split + (j + 1) * ny, :]

    narrow, wide = lo1, lo2
    row1 = places[0][0]
    for k, used in enumerate(taps[0]):
        acc = None
        for i in used:
            term = maps_ref[row1 + k, i] * one_slab(i)
            acc = term if acc is None else acc + term
        one_out[k * slab : (k + 1) * slab, :] = acc
        for b in range(2):
            at = (k * 2 + b) * narrow
            top_out[at : at + narrow, :] = acc[b * ny + ny - narrow : (b + 1) * ny, :]
            bottom_out[at : at + narrow, :] = acc[b * ny : b * ny + narrow, :]
    base = len(taps[0]) * 2 * narrow
    row2 = places[1][0]
    for k, used in enumerate(taps[1]):
        acc = None
        for i in used:
            term = maps_ref[row2 + k, i] * two_slab(i)
            acc = term if acc is None else acc + term
        two_out[k * ny : (k + 1) * ny, :] = acc
        top_out[base + k * wide : base + (k + 1) * wide, :] = acc[ny - wide :, :]
        bottom_out[base + k * wide : base + (k + 1) * wide, :] = acc[:wide, :]


def used_taps(maps):
    present = np.any(np.stack([m != 0 for m in maps]), axis=0)
    return tuple(tuple(int(i) for i in np.nonzero(row)[0]) for row in present)


def x_pass(edge, middle, coarse, below, above, x_maps, places, nx, ny):
    lanes = coarse.shape[-1]
    taps = (used_taps(window_maps(nx, (4, 4), 0)), used_taps(window_maps(nx, (12, 12), 1)))
    narrow, wide = 4, 12
    vmem = pl.BlockSpec(memory_space=pltpu.VMEM)
    smem = pl.BlockSpec(memory_space=pltpu.SMEM)
    message = len(taps[0]) * 2 * narrow + len(taps[1]) * wide
    return pl.pallas_call(
        functools.partial(x_pass_kernel, taps=taps, places=tuple(places)),
        out_shape=(
            jax.ShapeDtypeStruct((len(taps[0]) * 2 * ny, lanes), jnp.float32),
            jax.ShapeDtypeStruct((len(taps[1]) * ny, lanes), jnp.float32),
            jax.ShapeDtypeStruct((message, lanes), jnp.float32),
            jax.ShapeDtypeStruct((message, lanes), jnp.float32),
        ),
        in_specs=[vmem, vmem, vmem, vmem, vmem, smem],
        out_specs=(vmem, vmem, vmem, vmem),
    )(
        edge.reshape(-1, lanes), middle.reshape(-1, lanes), coarse.reshape(-1, lanes), below, above, x_maps
    )


def per_device(velocity):
    nx, ny, nz = velocity.shape

    (z_low, z_high), (z2_low, z2_high) = level_maps(nz)
    z_maps = np.stack([z_low.T, z_high.T, np.concatenate([z2_low, z2_high]).T]).astype(np.float32)
    lanes = z_maps.shape[2]
    wide = 12
    flat = lambda a: a.reshape(-1, lanes)
    coarse = jnp.einsum("xyz,zk->xyk", velocity, jnp.asarray(z_maps[2]), precision=EXACT)
    rims = jnp.concatenate([velocity[:4], velocity[nx - 4 :]])
    edge = jnp.einsum("xyz,bzk->xbyk", rims, jnp.asarray(z_maps[0:2]), precision=EXACT)
    top = jnp.concatenate([flat(edge[4:]), flat(coarse[nx - wide :])])
    bottom = jnp.concatenate([flat(edge[:4]), flat(coarse[:wide])])
    below, above = exchange(bottom, top, "slab")
    assert nx == ny and wide == 12
    table, places = packed_maps(nx)
    table = jnp.asarray(table)
    x_maps = lax.dynamic_index_in_dim(table, case_of("slab"), keepdims=False)
    y_maps = lax.dynamic_index_in_dim(table, case_of("morton"), keepdims=False)
    middle = jnp.einsum("xyz,bzk->xbyk", velocity[4 : nx - 4], jnp.asarray(z_maps[0:2]), precision=EXACT)
    x_one, x_two, top, bottom = x_pass(edge, middle, coarse, below, above, x_maps, places, nx, ny)

    below, above = exchange(bottom, top, "morton")
    return y_pass(x_one, x_two, below, above, y_maps, places, nx, ny, nz)


def solution(mesh):
    placed = (P("slab", "morton", None),)
    return jax.shard_map(
        per_device,
        mesh=mesh,
        in_specs=placed,
        out_specs=(
            P("slab", "morton", None),
            P(None, "slab", "morton", None),
            P(None, "slab", "morton", None),
        ),
        check_vma=False,
    )
```

```python
import functools

import numpy as np
import jax
import jax.numpy as jnp
from jax import lax
from jax.sharding import PartitionSpec as P
from jax.experimental import pallas as pl
from jax.experimental.pallas import tpu as pltpu

LIFT_ALPHA = -1.586134342059924
LIFT_BETA = -0.052980118572961
LIFT_GAMMA = 0.882911075530934
LIFT_DELTA = 0.443506852043971
LIFT_SCALE = 1.149604398860241

EXACT = lax.Precision.HIGHEST


def lift_rows(signal):
    extended = np.pad(signal, ((4, 4), (0, 0)), mode="reflect")
    even, odd = extended[0::2], extended[1::2]
    first_detail = odd[:-1] + LIFT_ALPHA * (even[:-1] + even[1:])
    first_smooth = even[1:-1] + LIFT_BETA * (first_detail[:-1] + first_detail[1:])
    second_detail = first_detail[1:-1] + LIFT_GAMMA * (first_smooth[:-1] + first_smooth[1:])
    second_smooth = first_smooth[1:-1] + LIFT_DELTA * (second_detail[:-1] + second_detail[1:])
    return second_smooth * LIFT_SCALE, second_detail[1:] / LIFT_SCALE


def level_maps(length):
    low, high = lift_rows(np.eye(length))
    low_two, high_two = lift_rows(low)
    return (low, high), (low_two, high_two)


def window_maps(block, halo, level, blocks=8):
    length = block * blocks
    bands = level_maps(length)[level]
    share = block // (2 * (level + 1))
    width = halo[0] + block + halo[1]
    maps = []
    for place in (0, blocks // 2, blocks - 1):
        rows = np.concatenate([band[place * share : (place + 1) * share] for band in bands])
        matrix = np.zeros((rows.shape[0], width))
        for i in range(width):
            cell = place * block - halo[0] + i
            if 0 <= cell < length:
                matrix[:, i] = rows[:, cell]
        maps.append(matrix.astype(np.float32))
    return maps


def packed_maps(block):
    parts = [
        window_maps(block, (4, 4), 0),
        window_maps(block, (12, 12), 1),
        window_maps(block, (8, 8), 0),
        window_maps(block, (block, block), 1),
    ]
    height = sum(p[0].shape[0] for p in parts)
    width = -(-max(p[0].shape[1] for p in parts) // 128) * 128
    table = np.zeros((3, height, width), np.float32)
    places, row = [], 0
    for p in parts:
        rows, cols = p[0].shape
        for case in range(3):
            table[case, row : row + rows, :cols] = p[case]
        places.append((row, rows, cols))
        row += rows
    return table, places


def case_of(axis):
    index = lax.axis_index(axis)
    last = lax.axis_size(axis) - 1
    return jnp.where(index == 0, 0, jnp.where(index == last, 2, 1))


def exchange(lower_half, upper_half, axis):
    devices = lax.axis_size(axis)
    up = [(i, i + 1) for i in range(devices - 1)]
    down = [(i + 1, i) for i in range(devices - 1)]
    from_below = lax.ppermute(upper_half, axis, up)
    from_above = lax.ppermute(lower_half, axis, down)
    return from_below, from_above


def y_pass_kernel(one_ref, two_ref, below_ref, above_ref, maps_ref, approx_ref, two_out, one_out, *, places):
    n_two, lanes = two_ref.shape
    n_one = one_ref.shape[0]
    ny = 2 * one_out.shape[2]
    slabs_one = n_one // ny
    slabs_two = n_two // ny
    narrow, wide = 4, 12
    blocks = []
    for s in range(slabs_one):
        blocks.append(
            jnp.concatenate(
                [
                    below_ref[s * narrow : (s + 1) * narrow, :],
                    one_ref[s * ny : (s + 1) * ny, :],
                    above_ref[s * narrow : (s + 1) * narrow, :],
                ]
            )
        )
    row, rows, cols = places[0]
    a1 = maps_ref[row : row + rows, :][:, :cols]
    result = jnp.dot(a1, jnp.concatenate(blocks, axis=1), precision=EXACT,
                     preferred_element_type=jnp.float32)
    half_x, half_y = one_out.shape[1], one_out.shape[2]
    for s in range(slabs_one):
        kx, bz = divmod(s, 2)
        bx, kx8 = divmod(kx, half_x)
        block = result[:, s * lanes : (s + 1) * lanes]
        for by in range(2):
            band = 4 * bx + 2 * by + bz
            if band:
                one_out[band - 1, kx8] = block[by * half_y : (by + 1) * half_y]
    base = n_one // ny * narrow
    blocks = []
    for s in range(slabs_two):
        blocks.append(
            jnp.concatenate(
                [
                    below_ref[base + s * wide : base + (s + 1) * wide, :],
                    two_ref[s * ny : (s + 1) * ny, :],
                    above_ref[base + s * wide : base + (s + 1) * wide, :],
                ]
            )
        )
    row, rows, cols = places[1]
    a2 = maps_ref[row : row + rows, :][:, :cols]
    result = jnp.dot(a2, jnp.concatenate(blocks, axis=1), precision=EXACT,
                     preferred_element_type=jnp.float32)
    quarter_x, quarter_y, quarter_z = approx_ref.shape
    for s in range(slabs_two):
        bx, kx4 = divmod(s, quarter_x)
        block = result[:, s * lanes : (s + 1) * lanes]
        for by in range(2):
            for bz in range(2):
                piece = block[by * quarter_y : (by + 1) * quarter_y, bz * quarter_z : (bz + 1) * quarter_z]
                band = 4 * bx + 2 * by + bz
                if band:
                    two_out[band - 1, kx4] = piece
                else:
                    approx_ref[kx4] = piece


def y_pass(x_one, x_two, below, above, y_maps, places, nx, ny, nz):
    vmem = pl.BlockSpec(memory_space=pltpu.VMEM)
    lanes = x_one.shape[-1]
    return pl.pallas_call(
        functools.partial(y_pass_kernel, places=tuple(places)),
        out_shape=(
            jax.ShapeDtypeStruct((nx // 4, ny // 4, nz // 4), jnp.float32),
            jax.ShapeDtypeStruct((7, nx // 4, ny // 4, nz // 4), jnp.float32),
            jax.ShapeDtypeStruct((7, nx // 2, ny // 2, lanes), jnp.float32),
        ),
        in_specs=[vmem] * 5,
        out_specs=(vmem, vmem, vmem),
    )(x_one.reshape(-1, lanes), x_two.reshape(-1, lanes), below, above, y_maps)


def x_pass_kernel(own_ref, below_hbm, above_hbm, maps_ref, one_out, two_out, top_out, bottom_out,
                  below_ref, above_ref, sems, *, taps, places, bands):
    fetch_below = pltpu.make_async_copy(below_hbm, below_ref, sems.at[0])
    fetch_above = pltpu.make_async_copy(above_hbm, above_ref, sems.at[1])
    fetch_below.start()
    fetch_above.start()
    ny = two_out.shape[0] // len(taps[1])
    slab = 2 * ny
    stride = bands * ny
    lo1, lo2 = 4, 12
    split = lo1 * slab

    def one_slab(i):
        if i < lo1:
            return below_ref[i * slab : (i + 1) * slab, :]
        if i < lo1 + ny:
            return own_ref[(i - lo1) * stride : (i - lo1) * stride + slab, :]
        j = i - lo1 - ny
        return above_ref[j * slab : (j + 1) * slab, :]

    def two_slab(i):
        if i < lo2:
            return below_ref[split + i * ny : split + (i + 1) * ny, :]
        if i < lo2 + ny:
            at = (i - lo2) * stride + slab
            return own_ref[at : at + ny, :]
        j = i - lo2 - ny
        return above_ref[split + j * ny : split + (j + 1) * ny, :]

    def weighted(row, used, piece, inside, acc):
        for i in used:
            if inside(i):
                term = maps_ref[row, i] * piece(i)
                acc = term if acc is None else acc + term
        return acc

    row1, row2 = places[0][0], places[1][0]
    own_one = lambda i: lo1 <= i < lo1 + ny
    own_two = lambda i: lo2 <= i < lo2 + ny
    lanes = own_ref.shape[1]
    for k, used in enumerate(taps[0]):
        acc = weighted(row1 + k, used, one_slab, own_one, None)
        one_out[k * slab : (k + 1) * slab, :] = acc if acc is not None else jnp.zeros((slab, lanes), jnp.float32)
    for k, used in enumerate(taps[1]):
        acc = weighted(row2 + k, used, two_slab, own_two, None)
        two_out[k * ny : (k + 1) * ny, :] = acc if acc is not None else jnp.zeros((ny, lanes), jnp.float32)
    fetch_below.wait()
    fetch_above.wait()

    narrow, wide = lo1, lo2
    for k, used in enumerate(taps[0]):
        acc = weighted(row1 + k, used, one_slab, lambda i: not own_one(i), one_out[k * slab : (k + 1) * slab, :])
        one_out[k * slab : (k + 1) * slab, :] = acc
        for b in range(2):
            at = (k * 2 + b) * narrow
            top_out[at : at + narrow, :] = acc[b * ny + ny - narrow : (b + 1) * ny, :]
            bottom_out[at : at + narrow, :] = acc[b * ny : b * ny + narrow, :]
    base = len(taps[0]) * 2 * narrow
    for k, used in enumerate(taps[1]):
        acc = weighted(row2 + k, used, two_slab, lambda i: not own_two(i), two_out[k * ny : (k + 1) * ny, :])
        two_out[k * ny : (k + 1) * ny, :] = acc
        top_out[base + k * wide : base + (k + 1) * wide, :] = acc[ny - wide :, :]
        bottom_out[base + k * wide : base + (k + 1) * wide, :] = acc[:wide, :]


def used_taps(maps):
    present = np.any(np.stack([m != 0 for m in maps]), axis=0)
    return tuple(tuple(int(i) for i in np.nonzero(row)[0]) for row in present)


def x_pass(u, below, above, x_maps, places, nx, ny):
    lanes = u.shape[-1]
    taps = (used_taps(window_maps(nx, (4, 4), 0)), used_taps(window_maps(nx, (12, 12), 1)))
    narrow, wide = 4, 12
    vmem = pl.BlockSpec(memory_space=pltpu.VMEM)
    smem = pl.BlockSpec(memory_space=pltpu.SMEM)
    message = len(taps[0]) * 2 * narrow + len(taps[1]) * wide
    return pl.pallas_call(
        functools.partial(x_pass_kernel, taps=taps, places=tuple(places), bands=u.shape[1]),
        out_shape=(
            jax.ShapeDtypeStruct((len(taps[0]) * 2 * ny, lanes), jnp.float32),
            jax.ShapeDtypeStruct((len(taps[1]) * ny, lanes), jnp.float32),
            jax.ShapeDtypeStruct((message, lanes), jnp.float32),
            jax.ShapeDtypeStruct((message, lanes), jnp.float32),
        ),
        in_specs=[vmem, pl.BlockSpec(memory_space=pl.ANY), pl.BlockSpec(memory_space=pl.ANY), smem],
        out_specs=(vmem, vmem, vmem, vmem),
        scratch_shapes=[
            pltpu.VMEM(below.shape, jnp.float32),
            pltpu.VMEM(above.shape, jnp.float32),
            pltpu.SemaphoreType.DMA((2,)),
        ],
    )(u.reshape(-1, lanes), below, above, x_maps)


def per_device(velocity):
    nx, ny, nz = velocity.shape

    (z_low, z_high), (z2_low, z2_high) = level_maps(nz)
    z_maps = np.stack([z_low.T, z_high.T, np.concatenate([z2_low, z2_high]).T]).astype(np.float32)
    lanes = z_maps.shape[2]
    u = jnp.einsum("xyz,bzk->xbyk", velocity, jnp.asarray(z_maps), precision=EXACT)

    wide = 12
    one_rows = u[:, 0:2]
    two_rows = u[:, 2]
    flat = lambda a: a.reshape(-1, lanes)
    top = jnp.concatenate([flat(one_rows[nx - 4 :]), flat(two_rows[nx - wide :])])
    bottom = jnp.concatenate([flat(one_rows[:4]), flat(two_rows[:wide])])
    below, above = exchange(bottom, top, "slab")
    assert nx == ny and wide == 12
    table, places = packed_maps(nx)
    table = jnp.asarray(table)
    x_maps = lax.dynamic_index_in_dim(table, case_of("slab"), keepdims=False)
    y_maps = lax.dynamic_index_in_dim(table, case_of("morton"), keepdims=False)
    x_one, x_two, top, bottom = x_pass(u, below, above, x_maps, places, nx, ny)

    below, above = exchange(bottom, top, "morton")
    return y_pass(x_one, x_two, below, above, y_maps, places, nx, ny, nz)


def solution(mesh):
    placed = (P("slab", "morton", None),)
    return jax.shard_map(
        per_device,
        mesh=mesh,
        in_specs=placed,
        out_specs=(
            P("slab", "morton", None),
            P(None, "slab", "morton", None),
            P(None, "slab", "morton", None),
        ),
        check_vma=False,
    )
```

```python
import functools

import numpy as np
import jax
import jax.numpy as jnp
from jax import lax
from jax.sharding import PartitionSpec as P
from jax.experimental import pallas as pl
from jax.experimental.pallas import tpu as pltpu

LIFT_ALPHA = -1.586134342059924
LIFT_BETA = -0.052980118572961
LIFT_GAMMA = 0.882911075530934
LIFT_DELTA = 0.443506852043971
LIFT_SCALE = 1.149604398860241

EXACT = lax.Precision.HIGHEST


def lift_rows(signal):
    extended = np.pad(signal, ((4, 4), (0, 0)), mode="reflect")
    even, odd = extended[0::2], extended[1::2]
    first_detail = odd[:-1] + LIFT_ALPHA * (even[:-1] + even[1:])
    first_smooth = even[1:-1] + LIFT_BETA * (first_detail[:-1] + first_detail[1:])
    second_detail = first_detail[1:-1] + LIFT_GAMMA * (first_smooth[:-1] + first_smooth[1:])
    second_smooth = first_smooth[1:-1] + LIFT_DELTA * (second_detail[:-1] + second_detail[1:])
    return second_smooth * LIFT_SCALE, second_detail[1:] / LIFT_SCALE


def level_maps(length):
    low, high = lift_rows(np.eye(length))
    low_two, high_two = lift_rows(low)
    return (low, high), (low_two, high_two)


def window_maps(block, halo, level, blocks=8):
    length = block * blocks
    bands = level_maps(length)[level]
    share = block // (2 * (level + 1))
    width = halo[0] + block + halo[1]
    maps = []
    for place in (0, blocks // 2, blocks - 1):
        rows = np.concatenate([band[place * share : (place + 1) * share] for band in bands])
        matrix = np.zeros((rows.shape[0], width))
        for i in range(width):
            cell = place * block - halo[0] + i
            if 0 <= cell < length:
                matrix[:, i] = rows[:, cell]
        maps.append(matrix.astype(np.float32))
    return maps


def packed_maps(block):
    parts = [
        window_maps(block, (4, 4), 0),
        window_maps(block, (12, 12), 1),
    ]
    height = sum(p[0].shape[0] for p in parts)
    width = -(-max(p[0].shape[1] for p in parts) // 128) * 128
    table = np.zeros((3, height, width), np.float32)
    places, row = [], 0
    for p in parts:
        rows, cols = p[0].shape
        for case in range(3):
            table[case, row : row + rows, :cols] = p[case]
        places.append((row, rows, cols))
        row += rows
    return table, places


def case_of(axis):
    index = lax.axis_index(axis)
    last = lax.axis_size(axis) - 1
    return jnp.where(index == 0, 0, jnp.where(index == last, 2, 1))


def exchange(lower_half, upper_half, axis):
    devices = lax.axis_size(axis)
    up = [(i, i + 1) for i in range(devices - 1)]
    down = [(i + 1, i) for i in range(devices - 1)]
    from_below = lax.ppermute(upper_half, axis, up)
    from_above = lax.ppermute(lower_half, axis, down)
    return from_below, from_above


def y_pass_kernel(one_ref, two_ref, below_ref, above_ref, maps_ref, approx_ref, two_out, one_out, *, places):
    n_two, lanes = two_ref.shape
    n_one = one_ref.shape[0]
    ny = 2 * one_out.shape[2]
    slabs_one = n_one // ny
    slabs_two = n_two // ny
    narrow, wide = 4, 12
    blocks = []
    for s in range(slabs_one):
        blocks.append(
            jnp.concatenate(
                [
                    below_ref[s * narrow : (s + 1) * narrow, :],
                    one_ref[s * ny : (s + 1) * ny, :],
                    above_ref[s * narrow : (s + 1) * narrow, :],
                ]
            )
        )
    row, rows, cols = places[0]
    a1 = maps_ref[row : row + rows, :][:, :cols]
    result = jnp.dot(a1, jnp.concatenate(blocks, axis=1), precision=EXACT,
                     preferred_element_type=jnp.float32)
    half_x, half_y = one_out.shape[1], one_out.shape[2]
    for s in range(slabs_one):
        kx, bz = divmod(s, 2)
        bx, kx8 = divmod(kx, half_x)
        block = result[:, s * lanes : (s + 1) * lanes]
        for by in range(2):
            band = 4 * bx + 2 * by + bz
            if band:
                one_out[band - 1, kx8] = block[by * half_y : (by + 1) * half_y]
    base = n_one // ny * narrow
    blocks = []
    for s in range(slabs_two):
        blocks.append(
            jnp.concatenate(
                [
                    below_ref[base + s * wide : base + (s + 1) * wide, :],
                    two_ref[s * ny : (s + 1) * ny, :],
                    above_ref[base + s * wide : base + (s + 1) * wide, :],
                ]
            )
        )
    row, rows, cols = places[1]
    a2 = maps_ref[row : row + rows, :][:, :cols]
    result = jnp.dot(a2, jnp.concatenate(blocks, axis=1), precision=EXACT,
                     preferred_element_type=jnp.float32)
    quarter_x, quarter_y, quarter_z = approx_ref.shape
    for s in range(slabs_two):
        bx, kx4 = divmod(s, quarter_x)
        block = result[:, s * lanes : (s + 1) * lanes]
        for by in range(2):
            for bz in range(2):
                piece = block[by * quarter_y : (by + 1) * quarter_y, bz * quarter_z : (bz + 1) * quarter_z]
                band = 4 * bx + 2 * by + bz
                if band:
                    two_out[band - 1, kx4] = piece
                else:
                    approx_ref[kx4] = piece


def y_pass(x_one, x_two, below, above, y_maps, places, nx, ny, nz):
    vmem = pl.BlockSpec(memory_space=pltpu.VMEM)
    lanes = x_one.shape[-1]
    return pl.pallas_call(
        functools.partial(y_pass_kernel, places=tuple(places)),
        out_shape=(
            jax.ShapeDtypeStruct((nx // 4, ny // 4, nz // 4), jnp.float32),
            jax.ShapeDtypeStruct((7, nx // 4, ny // 4, nz // 4), jnp.float32),
            jax.ShapeDtypeStruct((7, nx // 2, ny // 2, lanes), jnp.float32),
        ),
        in_specs=[vmem] * 5,
        out_specs=(vmem, vmem, vmem),
    )(x_one.reshape(-1, lanes), x_two.reshape(-1, lanes), below, above, y_maps)


def x_pass_kernel(own_ref, below_ref, above_ref, maps_ref, one_out, two_out, top_out, bottom_out, *,
                  taps, places, bands):
    ny = two_out.shape[0] // len(taps[1])
    slab = 2 * ny
    stride = bands * ny
    lo1, lo2 = 4, 12
    split = lo1 * slab

    def one_slab(i):
        if i < lo1:
            return below_ref[i * slab : (i + 1) * slab, :]
        if i < lo1 + ny:
            return own_ref[(i - lo1) * stride : (i - lo1) * stride + slab, :]
        j = i - lo1 - ny
        return above_ref[j * slab : (j + 1) * slab, :]

    def two_slab(i):
        if i < lo2:
            return below_ref[split + i * ny : split + (i + 1) * ny, :]
        if i < lo2 + ny:
            at = (i - lo2) * stride + slab
            return own_ref[at : at + ny, :]
        j = i - lo2 - ny
        return above_ref[split + j * ny : split + (j + 1) * ny, :]

    narrow, wide = lo1, lo2
    row1 = places[0][0]
    for k, used in enumerate(taps[0]):
        acc = None
        for i in used:
            term = maps_ref[row1 + k, i] * one_slab(i)
            acc = term if acc is None else acc + term
        one_out[k * slab : (k + 1) * slab, :] = acc
        for b in range(2):
            at = (k * 2 + b) * narrow
            top_out[at : at + narrow, :] = acc[b * ny + ny - narrow : (b + 1) * ny, :]
            bottom_out[at : at + narrow, :] = acc[b * ny : b * ny + narrow, :]
    base = len(taps[0]) * 2 * narrow
    row2 = places[1][0]
    for k, used in enumerate(taps[1]):
        acc = None
        for i in used:
            term = maps_ref[row2 + k, i] * two_slab(i)
            acc = term if acc is None else acc + term
        two_out[k * ny : (k + 1) * ny, :] = acc
        top_out[base + k * wide : base + (k + 1) * wide, :] = acc[ny - wide :, :]
        bottom_out[base + k * wide : base + (k + 1) * wide, :] = acc[:wide, :]


def used_taps(maps):
    present = np.any(np.stack([m != 0 for m in maps]), axis=0)
    return tuple(tuple(int(i) for i in np.nonzero(row)[0]) for row in present)


def x_pass(u, below, above, x_maps, places, nx, ny):
    lanes = u.shape[-1]
    taps = (used_taps(window_maps(nx, (4, 4), 0)), used_taps(window_maps(nx, (12, 12), 1)))
    narrow, wide = 4, 12
    vmem = pl.BlockSpec(memory_space=pltpu.VMEM)
    smem = pl.BlockSpec(memory_space=pltpu.SMEM)
    message = len(taps[0]) * 2 * narrow + len(taps[1]) * wide
    return pl.pallas_call(
        functools.partial(x_pass_kernel, taps=taps, places=tuple(places), bands=u.shape[1]),
        out_shape=(
            jax.ShapeDtypeStruct((len(taps[0]) * 2 * ny, lanes), jnp.float32),
            jax.ShapeDtypeStruct((len(taps[1]) * ny, lanes), jnp.float32),
            jax.ShapeDtypeStruct((message, lanes), jnp.float32),
            jax.ShapeDtypeStruct((message, lanes), jnp.float32),
        ),
        in_specs=[vmem, vmem, vmem, smem],
        out_specs=(vmem, vmem, vmem, vmem),
    )(u.reshape(-1, lanes), below, above, x_maps)


def per_device(velocity):
    nx, ny, nz = velocity.shape

    (z_low, z_high), (z2_low, z2_high) = level_maps(nz)
    z_maps = np.stack([z_low.T, z_high.T, np.concatenate([z2_low, z2_high]).T]).astype(np.float32)
    lanes = z_maps.shape[2]
    u = jnp.einsum("xyz,bzk->xbyk", velocity, jnp.asarray(z_maps), precision=EXACT)

    wide = 12
    one_rows = u[:, 0:2]
    two_rows = u[:, 2]
    flat = lambda a: a.reshape(-1, lanes)
    top = jnp.concatenate([flat(one_rows[nx - 4 :]), flat(two_rows[nx - wide :])])
    bottom = jnp.concatenate([flat(one_rows[:4]), flat(two_rows[:wide])])
    below, above = exchange(bottom, top, "slab")
    assert nx == ny and wide == 12
    table, places = packed_maps(nx)
    table = jnp.asarray(table)
    x_maps = lax.dynamic_index_in_dim(table, case_of("slab"), keepdims=False)
    y_maps = lax.dynamic_index_in_dim(table, case_of("morton"), keepdims=False)
    x_one, x_two, top, bottom = x_pass(u, below, above, x_maps, places, nx, ny)

    below, above = exchange(bottom, top, "morton")
    return y_pass(x_one, x_two, below, above, y_maps, places, nx, ny, nz)


def solution(mesh):
    placed = (P("slab", "morton", None),)
    return jax.shard_map(
        per_device,
        mesh=mesh,
        in_specs=placed,
        out_specs=(
            P("slab", "morton", None),
            P(None, "slab", "morton", None),
            P(None, "slab", "morton", None),
        ),
        check_vma=False,
    )
```
